32 devices in a mesh: grp: 2 (over y), outer: 4 (over x, core), inner: 4 (over z).
Axes of the slice: x: 2, y: 2, z: 4, core: 2. Of those that a mesh axis runs over, the one named last changes fastest.
Arguments:
- query: bfloat16 [4096, 1024], P(('grp', 'outer', 'inner')), parts along dimension 0, may hold values from -6 to 6
- key: bfloat16 [4096, 1024], P(('grp', 'outer', 'inner')), parts along dimension 0, may hold values from -6 to 6
- value: bfloat16 [4096, 1024], P(('grp', 'outer', 'inner')), parts along dimension 0, may hold values from -6 to 6
- grad_out: bfloat16 [4096, 1024], P(('grp', 'outer', 'inner')), parts along dimension 0, may hold values from -6 to 6
Outputs:
- normed_out: bfloat16 [4096, 1024], P(('grp', 'outer', 'inner')), parts along dimension 0
- grad_query: bfloat16 [4096, 1024], P(('grp', 'outer', 'inner')), parts along dimension 0
- grad_key: bfloat16 [4096, 1024], P(('grp', 'outer', 'inner')), parts along dimension 0
- grad_value: bfloat16 [4096, 1024], P(('grp', 'outer', 'inner')), parts along dimension 0
The draws below stay inside these ranges and needn't reach their ends.
There are 2 independent parts, one for each index of `grp`. The reference program is written for one: setup_inputs(seed, part) draws one part's arguments, and reference() takes and returns one part's arrays. A program takes and returns all parts, laid end to end along the dimension named above; each array names one. Nothing has to cross between parts.
All inputs are finite; a program needn't handle non-finite values.
Results may differ from the reference program's by a relative error of at most 0.0059.
Values sent between devices are 32-bit elements; how exact they have to be, the bound alone decides.
No kernel may reach another device: no remote copies, remote signals or barrier semaphores. Data moves between devices by JAX's collectives and lax.ppermute only.
A program may use at most 64 MiB of HBM per device.

```python
import jax
import jax.numpy as jnp
from jax import lax

HEADS = 8
HEAD = 128
TOK_DEV = 128
WIDTH = 1024
SEQ = 2048


def level_of(rng, extent, shards, low, high):
    loudness, own = 1.0, jax.random.fold_in(rng, 6)
    for dim, parts in shards:
        heights = jnp.exp(jax.random.uniform(jax.random.fold_in(own, dim), (parts,), jnp.float32, low / len(shards), high / len(shards)))
        loudness = loudness * jnp.repeat(heights, extent[dim] // parts).reshape([-1 if axis == dim else 1 for axis in range(len(extent))])
    return loudness


def normal_values(key, dims, width, reach, cuts=(), held_as=jnp.bfloat16):
    gain = level_of(key, dims, cuts, -0.22, 0.18) if cuts else 1.0
    values = jax.random.normal(key, dims, jnp.float32) * width * gain
    return jnp.minimum(jnp.maximum(values, -reach), reach).astype(held_as)


def setup_inputs(seed: int = 0, part: int = 0) -> dict:
    seeds = jax.random.split(jax.random.key(seed), 5)
    part_keys = jax.random.split(jax.random.fold_in(seeds[4], part), 5)
    query = normal_values(part_keys[0], (SEQ, WIDTH), 1.0, 6.0, ((0, 16),))
    key = normal_values(part_keys[1], (SEQ, WIDTH), 1.0, 6.0, ((0, 16),))
    value = normal_values(part_keys[2], (SEQ, WIDTH), 1.0, 6.0, ((0, 16),))
    grad_out = normal_values(part_keys[3], (SEQ, WIDTH), 1.0, 6.0, ((0, 16),))
    return dict(query=query, key=key, value=value, grad_out=grad_out)


def to_half(values):
    return lax.optimization_barrier(values.astype(jnp.bfloat16)).astype(jnp.float32)

def exclusive_prefix(states):
    running = jnp.cumsum(states, axis=0)
    empty_state = jnp.zeros_like(states[:1])
    return jnp.concatenate([empty_state, running[:-1]], axis=0)

def causal_mask(rows):
    line = lax.broadcasted_iota(jnp.int32, (rows, rows), 0)
    column = lax.broadcasted_iota(jnp.int32, (rows, rows), 1)
    return line >= column

def shaped(array, blocks):
    return array.astype(jnp.float32).reshape(blocks, TOK_DEV, HEADS, HEAD)

def reference(query, key, value, grad_out):
    blocks = SEQ // TOK_DEV
    scaling = HEAD ** (-0.5)
    queries = shaped(query, blocks)
    keys_all = shaped(key, blocks)
    values_all = shaped(value, blocks)
    grads_all = grad_out.astype(jnp.float32).reshape(blocks, TOK_DEV, WIDTH)
    states = jnp.einsum('nthi,nthj->nhij', keys_all, values_all)
    priors = exclusive_prefix(states)
    causal = causal_mask(TOK_DEV)[None]

    def half_scores(queries_b, keys_b):
        scores = jnp.einsum('thi,shi->hts', queries_b, keys_b) * scaling
        return to_half(jnp.where(causal, scores, 0.0))

    def half_dscores(grad_half, values_b):
        dscores = jnp.einsum('thj,shj->hts', grad_half, values_b)
        return to_half(jnp.where(causal, dscores, 0.0))

    def first_pass(items):
        queries_b, keys_b, values_b, grads_b, prior = items
        score_half = half_scores(queries_b, keys_b)
        prior_half = to_half(prior)
        attended = jnp.einsum('hts,shj->thj', score_half, values_b) + scaling * jnp.einsum('thi,hij->thj', queries_b, prior_half)
        flat = attended.reshape(TOK_DEV, WIDTH)
        inverse = lax.rsqrt(lax.optimization_barrier(jnp.mean(flat * flat, axis=-1, keepdims=True)) + 1e-05)
        normed = flat * inverse
        grad_pre = inverse * (grads_b - normed * lax.optimization_barrier(jnp.mean(grads_b * normed, axis=-1, keepdims=True)))
        grad_half = to_half(grad_pre).reshape(TOK_DEV, HEADS, HEAD)
        dscore_half = half_dscores(grad_half, values_b)
        grad_q = scaling * (jnp.einsum('hts,shi->thi', dscore_half, keys_b) + jnp.einsum('thj,hij->thi', grad_half, prior_half))
        grad_state = jnp.einsum('thi,thj->hij', queries_b, grad_half)
        return (normed.astype(jnp.bfloat16), grad_q.reshape(TOK_DEV, WIDTH).astype(jnp.bfloat16), grad_half, grad_state)
    normed_out, grad_query, grad_halves, grad_states = lax.map(first_pass, (queries, keys_all, values_all, grads_all, priors))
    laters = exclusive_prefix(grad_states[::-1])[::-1]

    def second_pass(items):
        queries_b, keys_b, values_b, grad_half, later = items
        score_half = half_scores(queries_b, keys_b)
        dscore_half = half_dscores(grad_half, values_b)
        later_half = to_half(later)
        grad_k = scaling * (jnp.einsum('hts,thi->shi', dscore_half, queries_b) + jnp.einsum('shj,hij->shi', values_b, later_half))
        grad_v = jnp.einsum('hts,thj->shj', score_half, grad_half) + scaling * jnp.einsum('shi,hij->shj', keys_b, later_half)
        return (grad_k.reshape(TOK_DEV, WIDTH).astype(jnp.bfloat16), grad_v.reshape(TOK_DEV, WIDTH).astype(jnp.bfloat16))
    grad_key, grad_value = lax.map(second_pass, (queries, keys_all, values_all, grad_halves, laters))
    return (normed_out.reshape(SEQ, WIDTH), grad_query.reshape(SEQ, WIDTH), grad_key.reshape(SEQ, WIDTH), grad_value.reshape(SEQ, WIDTH))
```

```python
import jax
import jax.numpy as jnp
from jax import lax
from jax.sharding import PartitionSpec as P

HEADS = 8
HEAD = 128


def hypercube_scan(value, backward):
    earlier = jnp.zeros_like(value)
    total = value
    for axis in ("inner", "outer"):
        count, mine = lax.axis_size(axis), lax.axis_index(axis)
        bit = 1
        while bit < count:
            pairs = [(i, i ^ bit) for i in range(count)]
            got = lax.ppermute(total, axis, pairs)
            partner_lower = (mine & bit) != 0
            take = jnp.logical_not(partner_lower) if backward else partner_lower
            earlier = jnp.where(take, earlier + got, earlier)
            total = total + got
            bit *= 2
    return earlier


def per_device(query, key, value, grad_out):
    rows_dev = query.shape[0]
    scaling = HEAD ** (-0.5)
    queries = query.reshape(rows_dev, HEADS, HEAD)
    key_rows = key.reshape(rows_dev, HEADS, HEAD)
    value_rows = value.reshape(rows_dev, HEADS, HEAD)
    line = lax.broadcasted_iota(jnp.int32, (rows_dev, rows_dev), 0)
    column = lax.broadcasted_iota(jnp.int32, (rows_dev, rows_dev), 1)
    causal = (line >= column)[None]
    state = jnp.einsum("thi,thj->hij", key_rows, value_rows, preferred_element_type=jnp.float32)
    prior = hypercube_scan(state, False)
    prior_half = prior.astype(jnp.bfloat16)
    scores = (
        jnp.einsum("thi,shi->hts", queries, key_rows, preferred_element_type=jnp.float32) * scaling
    )
    score_half = jnp.where(causal, scores, 0.0).astype(jnp.bfloat16)
    attended = jnp.einsum(
        "hts,shj->thj", score_half, value_rows, preferred_element_type=jnp.float32
    )
    attended = attended + scaling * jnp.einsum(
        "thi,hij->thj", queries, prior_half, preferred_element_type=jnp.float32
    )
    flat = attended.reshape(rows_dev, HEADS * HEAD)
    inverse = lax.rsqrt(jnp.mean(flat * flat, axis=-1, keepdims=True) + 1e-05)
    normed = flat * inverse
    grads_flat = grad_out.astype(jnp.float32)
    grad_pre = inverse * (
        grads_flat - normed * jnp.mean(grads_flat * normed, axis=-1, keepdims=True)
    )
    grad_half = grad_pre.astype(jnp.bfloat16).reshape(rows_dev, HEADS, HEAD)
    dscores = jnp.einsum("thj,shj->hts", grad_half, value_rows, preferred_element_type=jnp.float32)
    dscore_half = jnp.where(causal, dscores, 0.0).astype(jnp.bfloat16)
    grad_q = jnp.einsum("hts,shi->thi", dscore_half, key_rows, preferred_element_type=jnp.float32)
    grad_q = scaling * (
        grad_q
        + jnp.einsum("thj,hij->thi", grad_half, prior_half, preferred_element_type=jnp.float32)
    )
    grad_state = jnp.einsum("thi,thj->hij", queries, grad_half, preferred_element_type=jnp.float32)
    later = hypercube_scan(grad_state, True)
    later_half = later.astype(jnp.bfloat16)
    grad_k = jnp.einsum("hts,thi->shi", dscore_half, queries, preferred_element_type=jnp.float32)
    grad_k = scaling * (
        grad_k
        + jnp.einsum("shj,hij->shi", value_rows, later_half, preferred_element_type=jnp.float32)
    )
    grad_v = jnp.einsum("hts,thj->shj", score_half, grad_half, preferred_element_type=jnp.float32)
    grad_v = grad_v + scaling * jnp.einsum(
        "shi,hij->shj", key_rows, later_half, preferred_element_type=jnp.float32
    )
    width = HEADS * HEAD
    return (
        normed.astype(jnp.bfloat16),
        grad_q.reshape(rows_dev, width).astype(jnp.bfloat16),
        grad_k.reshape(rows_dev, width).astype(jnp.bfloat16),
        grad_v.reshape(rows_dev, width).astype(jnp.bfloat16),
    )


def solution(mesh):
    placed = P(("grp", "outer", "inner"), None)
    return jax.shard_map(
        per_device,
        mesh=mesh,
        in_specs=(placed, placed, placed, placed),
        out_specs=(placed, placed, placed, placed),
        check_vma=False,
    )
```

```python
import jax
import jax.numpy as jnp
from jax import lax
from jax.sharding import PartitionSpec as P

HEADS = 8
HEAD = 128


def axis_bits(axis):
    count = lax.axis_size(axis)
    return [1 << k for k in range(count.bit_length() - 1)]


def swap(value, axis, bit):
    count = lax.axis_size(axis)
    return lax.ppermute(value, axis, [(i, i ^ bit) for i in range(count)])


def partner_counts(axis, bit, backward):
    partner_lower = (lax.axis_index(axis) & bit) != 0
    return jnp.logical_not(partner_lower) if backward else partner_lower


def subcube_step(earlier, total, axis, bit, backward):
    got = swap(total, axis, bit)
    earlier = jnp.where(partner_counts(axis, bit, backward), earlier + got, earlier)
    return earlier, total + got


def scan_inner_first(value, backward):
    earlier, total = jnp.zeros_like(value), value
    for axis in ("inner", "outer"):
        for bit in axis_bits(axis):
            earlier, total = subcube_step(earlier, total, axis, bit, backward)
    return earlier


def scan_outer_middle(value, backward):
    inner_bits = axis_bits("inner")
    if not inner_bits:
        return scan_inner_first(value, backward)
    earlier, total = jnp.zeros_like(value), value
    for bit in inner_bits[:-1]:
        earlier, total = subcube_step(earlier, total, "inner", bit, backward)
    rows_before, rows_total = jnp.zeros_like(value), total
    for bit in axis_bits("outer"):
        rows_before, rows_total = subcube_step(rows_before, rows_total, "outer", bit, backward)
    top = inner_bits[-1]
    counted = partner_counts("inner", top, backward)
    sent = jnp.where(counted, rows_before, rows_before + total)
    return rows_before + swap(sent, "inner", top) + earlier


def chunked_scan(value, backward):
    half = value.shape[0] // 2
    first = scan_inner_first(value[:half], backward)
    second = scan_outer_middle(value[half:], backward)
    return jnp.concatenate([first, second], axis=0)


def per_device(query, key, value, grad_out):
    rows_dev = query.shape[0]
    scaling = HEAD ** (-0.5)
    queries = query.reshape(rows_dev, HEADS, HEAD)
    key_rows = key.reshape(rows_dev, HEADS, HEAD)
    value_rows = value.reshape(rows_dev, HEADS, HEAD)
    line = lax.broadcasted_iota(jnp.int32, (rows_dev, rows_dev), 0)
    column = lax.broadcasted_iota(jnp.int32, (rows_dev, rows_dev), 1)
    causal = (line >= column)[None]
    state = jnp.einsum("thi,thj->hij", key_rows, value_rows, preferred_element_type=jnp.float32)
    prior = chunked_scan(state, False)
    prior_half = prior.astype(jnp.bfloat16)
    scores = (
        jnp.einsum("thi,shi->hts", queries, key_rows, preferred_element_type=jnp.float32) * scaling
    )
    score_half = jnp.where(causal, scores, 0.0).astype(jnp.bfloat16)
    attended = jnp.einsum(
        "hts,shj->thj", score_half, value_rows, preferred_element_type=jnp.float32
    )
    attended = attended + scaling * jnp.einsum(
        "thi,hij->thj", queries, prior_half, preferred_element_type=jnp.float32
    )
    flat = attended.reshape(rows_dev, HEADS * HEAD)
    inverse = lax.rsqrt(jnp.mean(flat * flat, axis=-1, keepdims=True) + 1e-05)
    normed = flat * inverse
    grads_flat = grad_out.astype(jnp.float32)
    grad_pre = inverse * (
        grads_flat - normed * jnp.mean(grads_flat * normed, axis=-1, keepdims=True)
    )
    grad_half = grad_pre.astype(jnp.bfloat16).reshape(rows_dev, HEADS, HEAD)
    dscores = jnp.einsum("thj,shj->hts", grad_half, value_rows, preferred_element_type=jnp.float32)
    dscore_half = jnp.where(causal, dscores, 0.0).astype(jnp.bfloat16)
    grad_q = jnp.einsum("hts,shi->thi", dscore_half, key_rows, preferred_element_type=jnp.float32)
    grad_q = scaling * (
        grad_q
        + jnp.einsum("thj,hij->thi", grad_half, prior_half, preferred_element_type=jnp.float32)
    )
    grad_state = jnp.einsum("thi,thj->hij", queries, grad_half, preferred_element_type=jnp.float32)
    later = chunked_scan(grad_state, True)
    later_half = later.astype(jnp.bfloat16)
    grad_k = jnp.einsum("hts,thi->shi", dscore_half, queries, preferred_element_type=jnp.float32)
    grad_k = scaling * (
        grad_k
        + jnp.einsum("shj,hij->shi", value_rows, later_half, preferred_element_type=jnp.float32)
    )
    grad_v = jnp.einsum("hts,thj->shj", score_half, grad_half, preferred_element_type=jnp.float32)
    grad_v = grad_v + scaling * jnp.einsum(
        "shi,hij->shj", key_rows, later_half, preferred_element_type=jnp.float32
    )
    width = HEADS * HEAD
    return (
        normed.astype(jnp.bfloat16),
        grad_q.reshape(rows_dev, width).astype(jnp.bfloat16),
        grad_k.reshape(rows_dev, width).astype(jnp.bfloat16),
        grad_v.reshape(rows_dev, width).astype(jnp.bfloat16),
    )


def solution(mesh):
    placed = P(("grp", "outer", "inner"), None)
    return jax.shard_map(
        per_device,
        mesh=mesh,
        in_specs=(placed, placed, placed, placed),
        out_specs=(placed, placed, placed, placed),
        check_vma=False,
    )
```

```python
import jax
import jax.numpy as jnp
from jax import lax
from jax.sharding import PartitionSpec as P

HEADS = 8
HEAD = 128


def axis_bits(axis):
    count = lax.axis_size(axis)
    return [1 << k for k in range(count.bit_length() - 1)]


def swap(value, axis, bit):
    count = lax.axis_size(axis)
    return lax.ppermute(value, axis, [(i, i ^ bit) for i in range(count)])


def partner_counts(axis, bit, backward):
    partner_lower = (lax.axis_index(axis) & bit) != 0
    return jnp.logical_not(partner_lower) if backward else partner_lower


def subcube_step(earlier, total, axis, bit, backward):
    got = swap(total, axis, bit)
    earlier = jnp.where(partner_counts(axis, bit, backward), earlier + got, earlier)
    return earlier, total + got


def scan_inner_first(value, backward):
    earlier, total = jnp.zeros_like(value), value
    for axis in ("inner", "outer"):
        for bit in axis_bits(axis):
            earlier, total = subcube_step(earlier, total, axis, bit, backward)
    return earlier


def scan_outer_middle(value, backward):
    inner_bits = axis_bits("inner")
    if not inner_bits:
        return scan_inner_first(value, backward)
    earlier, total = jnp.zeros_like(value), value
    for bit in inner_bits[:-1]:
        earlier, total = subcube_step(earlier, total, "inner", bit, backward)
    rows_before, rows_total = jnp.zeros_like(value), total
    for bit in axis_bits("outer"):
        rows_before, rows_total = subcube_step(rows_before, rows_total, "outer", bit, backward)
    top = inner_bits[-1]
    counted = partner_counts("inner", top, backward)
    sent = jnp.where(counted, rows_before, rows_before + total)
    return rows_before + swap(sent, "inner", top) + earlier


def chunked_scan(value, backward):
    half = value.shape[0] // 2
    if backward:
        first = scan_outer_middle(value[:half], backward)
        second = scan_inner_first(value[half:], backward)
    else:
        first = scan_inner_first(value[:half], backward)
        second = scan_outer_middle(value[half:], backward)
    return jnp.concatenate([first, second], axis=0)


def per_device(query, key, value, grad_out):
    rows_dev = query.shape[0]
    scaling = HEAD ** (-0.5)
    queries = query.reshape(rows_dev, HEADS, HEAD)
    key_rows = key.reshape(rows_dev, HEADS, HEAD)
    value_rows = value.reshape(rows_dev, HEADS, HEAD)
    line = lax.broadcasted_iota(jnp.int32, (rows_dev, rows_dev), 0)
    column = lax.broadcasted_iota(jnp.int32, (rows_dev, rows_dev), 1)
    causal = (line >= column)[None]
    state = jnp.einsum("thi,thj->hij", key_rows, value_rows, preferred_element_type=jnp.float32)
    prior = chunked_scan(state, False)
    prior_half = prior.astype(jnp.bfloat16)
    scores = (
        jnp.einsum("thi,shi->hts", queries, key_rows, preferred_element_type=jnp.float32) * scaling
    )
    score_half = jnp.where(causal, scores, 0.0).astype(jnp.bfloat16)
    attended = jnp.einsum(
        "hts,shj->thj", score_half, value_rows, preferred_element_type=jnp.float32
    )
    attended = attended + scaling * jnp.einsum(
        "thi,hij->thj", queries, prior_half, preferred_element_type=jnp.float32
    )
    flat = attended.reshape(rows_dev, HEADS * HEAD)
    inverse = lax.rsqrt(jnp.mean(flat * flat, axis=-1, keepdims=True) + 1e-05)
    normed = flat * inverse
    grads_flat = grad_out.astype(jnp.float32)
    grad_pre = inverse * (
        grads_flat - normed * jnp.mean(grads_flat * normed, axis=-1, keepdims=True)
    )
    grad_half = grad_pre.astype(jnp.bfloat16).reshape(rows_dev, HEADS, HEAD)
    dscores = jnp.einsum("thj,shj->hts", grad_half, value_rows, preferred_element_type=jnp.float32)
    dscore_half = jnp.where(causal, dscores, 0.0).astype(jnp.bfloat16)
    grad_q = jnp.einsum("hts,shi->thi", dscore_half, key_rows, preferred_element_type=jnp.float32)
    grad_q = scaling * (
        grad_q
        + jnp.einsum("thj,hij->thi", grad_half, prior_half, preferred_element_type=jnp.float32)
    )
    grad_state = jnp.einsum("thi,thj->hij", queries, grad_half, preferred_element_type=jnp.float32)
    later = chunked_scan(grad_state, True)
    later_half = later.astype(jnp.bfloat16)
    grad_k = jnp.einsum("hts,thi->shi", dscore_half, queries, preferred_element_type=jnp.float32)
    grad_k = scaling * (
        grad_k
        + jnp.einsum("shj,hij->shi", value_rows, later_half, preferred_element_type=jnp.float32)
    )
    grad_v = jnp.einsum("hts,thj->shj", score_half, grad_half, preferred_element_type=jnp.float32)
    grad_v = grad_v + scaling * jnp.einsum(
        "shi,hij->shj", key_rows, later_half, preferred_element_type=jnp.float32
    )
    width = HEADS * HEAD
    return (
        normed.astype(jnp.bfloat16),
        grad_q.reshape(rows_dev, width).astype(jnp.bfloat16),
        grad_k.reshape(rows_dev, width).astype(jnp.bfloat16),
        grad_v.reshape(rows_dev, width).astype(jnp.bfloat16),
    )


def solution(mesh):
    placed = P(("grp", "outer", "inner"), None)
    return jax.shard_map(
        per_device,
        mesh=mesh,
        in_specs=(placed, placed, placed, placed),
        out_specs=(placed, placed, placed, placed),
        check_vma=False,
    )
```

```python
import jax
import jax.numpy as jnp
from jax import lax
from jax.sharding import PartitionSpec as P

HEADS = 8
HEAD = 128


def axis_bits(axis):
    count = lax.axis_size(axis)
    return [1 << k for k in range(count.bit_length() - 1)]


def swap(value, axis, bit):
    count = lax.axis_size(axis)
    return lax.ppermute(value, axis, [(i, i ^ bit) for i in range(count)])


def partner_counts(axis, bit, backward):
    partner_lower = (lax.axis_index(axis) & bit) != 0
    return jnp.logical_not(partner_lower) if backward else partner_lower


def subcube_step(earlier, total, axis, bit, backward):
    got = swap(total, axis, bit)
    earlier = jnp.where(partner_counts(axis, bit, backward), earlier + got, earlier)
    return lax.optimization_barrier(earlier), total + got


def chunked_scan(value, backward):
    half = value.shape[0] // 2
    group_a, group_b = value[:half], value[half:]
    if backward:
        group_a, group_b = group_b, group_a
    inner_bits, outer_bits = axis_bits("inner"), axis_bits("outer")
    earlier_a, total_a = jnp.zeros_like(group_a), group_a
    earlier_b, total_b = jnp.zeros_like(group_b), group_b
    for bit in inner_bits[:-1]:
        earlier_a, total_a = subcube_step(earlier_a, total_a, "inner", bit, backward)
        earlier_b, total_b = subcube_step(earlier_b, total_b, "inner", bit, backward)
    rows_before, rows_total = jnp.zeros_like(group_b), total_b
    for index, bit in enumerate(outer_bits):
        rows_before, rows_total = subcube_step(rows_before, rows_total, "outer", bit, backward)
        if index == 0 and not backward:
            (earlier_a, total_a), _ = lax.optimization_barrier(((earlier_a, total_a), rows_total))
    for bit in inner_bits[-1:]:
        earlier_a, total_a = subcube_step(earlier_a, total_a, "inner", bit, backward)
    for bit in outer_bits:
        earlier_a, total_a = subcube_step(earlier_a, total_a, "outer", bit, backward)
    if inner_bits:
        top = inner_bits[-1]
        counted = partner_counts("inner", top, backward)
        sent = jnp.where(counted, rows_before, rows_before + total_b)
        earlier_b = rows_before + swap(sent, "inner", top) + earlier_b
    else:
        earlier_b = rows_before
    if backward:
        earlier_a, earlier_b = earlier_b, earlier_a
    return jnp.concatenate([earlier_a, earlier_b], axis=0)


def dot(left, right, contract):
    return lax.dot_general(
        left, right, ((contract[0], contract[1]), ((), ())), preferred_element_type=jnp.float32
    )


def per_device(query, key, value, grad_out):
    rows_dev = query.shape[0]
    scaling = HEAD ** (-0.5)
    line = lax.broadcasted_iota(jnp.int32, (rows_dev, rows_dev), 0)
    column = lax.broadcasted_iota(jnp.int32, (rows_dev, rows_dev), 1)
    causal = line >= column
    heads = [slice(h * HEAD, (h + 1) * HEAD) for h in range(HEADS)]
    queries = [query[:, c] for c in heads]
    keys = [key[:, c] for c in heads]
    values = [value[:, c] for c in heads]
    state = jnp.stack([dot(k, v, ((0,), (0,))) for k, v in zip(keys, values)])
    prior = chunked_scan(state, False)
    prior_half = prior.astype(jnp.bfloat16)
    score_half = [
        jnp.where(causal, dot(q, k, ((1,), (1,))) * scaling, 0.0).astype(jnp.bfloat16)
        for q, k in zip(queries, keys)
    ]
    attended = jnp.concatenate(
        [
            dot(s, v, ((1,), (0,))) + scaling * dot(q, p, ((1,), (0,)))
            for s, v, q, p in zip(score_half, values, queries, prior_half)
        ],
        axis=1,
    )
    inverse = lax.rsqrt(jnp.mean(attended * attended, axis=-1, keepdims=True) + 1e-05)
    normed = attended * inverse
    grads_flat = grad_out.astype(jnp.float32)
    grad_pre = inverse * (
        grads_flat - normed * jnp.mean(grads_flat * normed, axis=-1, keepdims=True)
    )
    grad_half = grad_pre.astype(jnp.bfloat16)
    grads = [grad_half[:, c] for c in heads]
    dscore_half = [
        jnp.where(causal, dot(g, v, ((1,), (1,))), 0.0).astype(jnp.bfloat16)
        for g, v in zip(grads, values)
    ]
    grad_q = jnp.concatenate(
        [
            scaling * (dot(d, k, ((1,), (0,))) + dot(g, p, ((1,), (1,))))
            for d, k, g, p in zip(dscore_half, keys, grads, prior_half)
        ],
        axis=1,
    )
    grad_state = jnp.stack([dot(q, g, ((0,), (0,))) for q, g in zip(queries, grads)])
    later = chunked_scan(grad_state, True)
    later_half = later.astype(jnp.bfloat16)
    grad_k = jnp.concatenate(
        [
            scaling * (dot(d, q, ((0,), (0,))) + dot(v, l, ((1,), (1,))))
            for d, q, v, l in zip(dscore_half, queries, values, later_half)
        ],
        axis=1,
    )
    grad_v = jnp.concatenate(
        [
            dot(s, g, ((0,), (0,))) + scaling * dot(k, l, ((1,), (0,)))
            for s, g, k, l in zip(score_half, grads, keys, later_half)
        ],
        axis=1,
    )
    return (
        normed.astype(jnp.bfloat16),
        grad_q.astype(jnp.bfloat16),
        grad_k.astype(jnp.bfloat16),
        grad_v.astype(jnp.bfloat16),
    )


def solution(mesh):
    placed = P(("grp", "outer", "inner"), None)
    return jax.shard_map(
        per_device,
        mesh=mesh,
        in_specs=(placed, placed, placed, placed),
        out_specs=(placed, placed, placed, placed),
        check_vma=False,
    )
```

```python
import jax
import jax.numpy as jnp
from jax import lax
from jax.sharding import PartitionSpec as P

HEADS = 8
HEAD = 128


def axis_bits(axis):
    count = lax.axis_size(axis)
    return [1 << k for k in range(count.bit_length() - 1)]


def swap(value, axis, bit):
    count = lax.axis_size(axis)
    return lax.ppermute(value, axis, [(i, i ^ bit) for i in range(count)])


def partner_counts(axis, bit, backward):
    partner_lower = (lax.axis_index(axis) & bit) != 0
    return jnp.logical_not(partner_lower) if backward else partner_lower


def subcube_step(earlier, total, axis, bit, backward):
    got = swap(total, axis, bit)
    earlier = jnp.where(partner_counts(axis, bit, backward), earlier + got, earlier)
    return lax.optimization_barrier(earlier), total + got


def chunked_scan(value, backward):
    half = value.shape[0] // 2
    group_a, group_b = value[:half], value[half:]
    if backward:
        group_a, group_b = group_b, group_a
    inner_bits, outer_bits = axis_bits("inner"), axis_bits("outer")
    earlier_a, total_a = jnp.zeros_like(group_a), group_a
    earlier_b, total_b = jnp.zeros_like(group_b), group_b
    for bit in inner_bits[:-1]:
        earlier_a, total_a = subcube_step(earlier_a, total_a, "inner", bit, backward)
        earlier_b, total_b = subcube_step(earlier_b, total_b, "inner", bit, backward)
    rows_before, rows_total = jnp.zeros_like(group_b), total_b
    for index, bit in enumerate(outer_bits):
        rows_before, rows_total = subcube_step(rows_before, rows_total, "outer", bit, backward)
        if index == 0 and not backward:
            (earlier_a, total_a), _ = lax.optimization_barrier(((earlier_a, total_a), rows_total))
    for bit in inner_bits[-1:]:
        earlier_a, total_a = subcube_step(earlier_a, total_a, "inner", bit, backward)
    for bit in outer_bits:
        earlier_a, total_a = subcube_step(earlier_a, total_a, "outer", bit, backward)
    if inner_bits:
        top = inner_bits[-1]
        counted = partner_counts("inner", top, backward)
        sent = jnp.where(counted, rows_before, rows_before + total_b)
        earlier_b = rows_before + swap(sent, "inner", top) + earlier_b
    else:
        earlier_b = rows_before
    if backward:
        earlier_a, earlier_b = earlier_b, earlier_a
    return jnp.concatenate([earlier_a, earlier_b], axis=0)


def per_device(query, key, value, grad_out):
    rows_dev = query.shape[0]
    scaling = HEAD ** (-0.5)
    queries = query.reshape(rows_dev, HEADS, HEAD)
    key_rows = key.reshape(rows_dev, HEADS, HEAD)
    value_rows = value.reshape(rows_dev, HEADS, HEAD)
    line = lax.broadcasted_iota(jnp.int32, (rows_dev, rows_dev), 0)
    column = lax.broadcasted_iota(jnp.int32, (rows_dev, rows_dev), 1)
    causal = (line >= column)[None]
    state = jnp.einsum("thi,thj->hij", key_rows, value_rows, preferred_element_type=jnp.float32)
    prior = chunked_scan(state, False)
    prior_half = prior.astype(jnp.bfloat16)
    scores = (
        jnp.einsum("thi,shi->hts", queries, key_rows, preferred_element_type=jnp.float32) * scaling
    )
    score_half = jnp.where(causal, scores, 0.0).astype(jnp.bfloat16)
    attended = jnp.einsum(
        "hts,shj->thj", score_half, value_rows, preferred_element_type=jnp.float32
    )
    attended = attended + scaling * jnp.einsum(
        "thi,hij->thj", queries, prior_half, preferred_element_type=jnp.float32
    )
    flat = attended.reshape(rows_dev, HEADS * HEAD)
    inverse = lax.rsqrt(jnp.mean(flat * flat, axis=-1, keepdims=True) + 1e-05)
    normed = flat * inverse
    grads_flat = grad_out.astype(jnp.float32)
    grad_pre = inverse * (
        grads_flat - normed * jnp.mean(grads_flat * normed, axis=-1, keepdims=True)
    )
    grad_half = grad_pre.astype(jnp.bfloat16).reshape(rows_dev, HEADS, HEAD)
    dscores = jnp.einsum("thj,shj->hts", grad_half, value_rows, preferred_element_type=jnp.float32)
    dscore_half = jnp.where(causal, dscores, 0.0).astype(jnp.bfloat16)
    grad_q = jnp.einsum("hts,shi->thi", dscore_half, key_rows, preferred_element_type=jnp.float32)
    grad_q = scaling * (
        grad_q
        + jnp.einsum("thj,hij->thi", grad_half, prior_half, preferred_element_type=jnp.float32)
    )
    grad_state = jnp.einsum("thi,thj->hij", queries, grad_half, preferred_element_type=jnp.float32)
    later = chunked_scan(grad_state, True)
    later_half = later.astype(jnp.bfloat16)
    grad_k = jnp.einsum("hts,thi->shi", dscore_half, queries, preferred_element_type=jnp.float32)
    grad_k = scaling * (
        grad_k
        + jnp.einsum("shj,hij->shi", value_rows, later_half, preferred_element_type=jnp.float32)
    )
    grad_v = jnp.einsum("hts,thj->shj", score_half, grad_half, preferred_element_type=jnp.float32)
    grad_v = grad_v + scaling * jnp.einsum(
        "shi,hij->shj", key_rows, later_half, preferred_element_type=jnp.float32
    )
    width = HEADS * HEAD
    return (
        normed.astype(jnp.bfloat16),
        grad_q.reshape(rows_dev, width).astype(jnp.bfloat16),
        grad_k.reshape(rows_dev, width).astype(jnp.bfloat16),
        grad_v.reshape(rows_dev, width).astype(jnp.bfloat16),
    )


def solution(mesh):
    placed = P(("grp", "outer", "inner"), None)
    return jax.shard_map(
        per_device,
        mesh=mesh,
        in_specs=(placed, placed, placed, placed),
        out_specs=(placed, placed, placed, placed),
        check_vma=False,
    )
```

```python
import jax
import jax.numpy as jnp
from jax import lax
from jax.sharding import PartitionSpec as P

HEADS = 8
HEAD = 128


def axis_bits(axis):
    count = lax.axis_size(axis)
    return [1 << k for k in range(count.bit_length() - 1)]


def swap(value, axis, bit):
    count = lax.axis_size(axis)
    return lax.ppermute(value, axis, [(i, i ^ bit) for i in range(count)])


def partner_counts(axis, bit, backward):
    partner_lower = (lax.axis_index(axis) & bit) != 0
    return jnp.logical_not(partner_lower) if backward else partner_lower


def subcube_step(earlier, total, axis, bit, backward):
    got = swap(total, axis, bit)
    earlier = jnp.where(partner_counts(axis, bit, backward), earlier + got, earlier)
    return earlier, total + got


def scan_inner_first(value, backward):
    earlier, total = jnp.zeros_like(value), value
    for axis in ("inner", "outer"):
        for bit in axis_bits(axis):
            earlier, total = subcube_step(earlier, total, axis, bit, backward)
    return earlier


def chunked_scan(value, backward):
    half = value.shape[0] // 2
    group_a, group_b = value[:half], value[half:]
    if backward:
        group_a, group_b = group_b, group_a
    inner_bits, outer_bits = axis_bits("inner"), axis_bits("outer")
    if not inner_bits:
        return scan_inner_first(value, backward)
    earlier_a, total_a = subcube_step(
        jnp.zeros_like(group_a), group_a, "inner", inner_bits[0], backward
    )
    earlier_b, total_b = jnp.zeros_like(group_b), group_b
    for bit in inner_bits[1:]:
        earlier_b, total_b = subcube_step(earlier_b, total_b, "inner", bit, backward)
    (earlier_b, total_b), _ = lax.optimization_barrier(((earlier_b, total_b), total_a))
    rows_before, rows_total = jnp.zeros_like(group_b), total_b
    for index, bit in enumerate(outer_bits):
        rows_before, rows_total = subcube_step(rows_before, rows_total, "outer", bit, backward)
        if index == 0:
            (earlier_a, total_a), _ = lax.optimization_barrier(((earlier_a, total_a), rows_total))
    for bit in inner_bits[1:]:
        earlier_a, total_a = subcube_step(earlier_a, total_a, "inner", bit, backward)
    for bit in outer_bits:
        earlier_a, total_a = subcube_step(earlier_a, total_a, "outer", bit, backward)
    low = inner_bits[0]
    counted = partner_counts("inner", low, backward)
    known = rows_before + earlier_b
    sent = jnp.where(counted, known, known + group_b)
    earlier_b = known + swap(sent, "inner", low)
    if backward:
        earlier_a, earlier_b = earlier_b, earlier_a
    return jnp.concatenate([earlier_a, earlier_b], axis=0)


def per_device(query, key, value, grad_out):
    rows_dev = query.shape[0]
    scaling = HEAD ** (-0.5)
    queries = query.reshape(rows_dev, HEADS, HEAD)
    key_rows = key.reshape(rows_dev, HEADS, HEAD)
    value_rows = value.reshape(rows_dev, HEADS, HEAD)
    line = lax.broadcasted_iota(jnp.int32, (rows_dev, rows_dev), 0)
    column = lax.broadcasted_iota(jnp.int32, (rows_dev, rows_dev), 1)
    causal = (line >= column)[None]
    state = jnp.einsum("thi,thj->hij", key_rows, value_rows, preferred_element_type=jnp.float32)
    prior = chunked_scan(state, False)
    prior_half = prior.astype(jnp.bfloat16)
    scores = (
        jnp.einsum("thi,shi->hts", queries, key_rows, preferred_element_type=jnp.float32) * scaling
    )
    score_half = jnp.where(causal, scores, 0.0).astype(jnp.bfloat16)
    attended = jnp.einsum(
        "hts,shj->thj", score_half, value_rows, preferred_element_type=jnp.float32
    )
    attended = attended + scaling * jnp.einsum(
        "thi,hij->thj", queries, prior_half, preferred_element_type=jnp.float32
    )
    flat = attended.reshape(rows_dev, HEADS * HEAD)
    inverse = lax.rsqrt(jnp.mean(flat * flat, axis=-1, keepdims=True) + 1e-05)
    normed = flat * inverse
    grads_flat = grad_out.astype(jnp.float32)
    grad_pre = inverse * (
        grads_flat - normed * jnp.mean(grads_flat * normed, axis=-1, keepdims=True)
    )
    grad_half = grad_pre.astype(jnp.bfloat16).reshape(rows_dev, HEADS, HEAD)
    dscores = jnp.einsum("thj,shj->hts", grad_half, value_rows, preferred_element_type=jnp.float32)
    dscore_half = jnp.where(causal, dscores, 0.0).astype(jnp.bfloat16)
    grad_q = jnp.einsum("hts,shi->thi", dscore_half, key_rows, preferred_element_type=jnp.float32)
    grad_q = scaling * (
        grad_q
        + jnp.einsum("thj,hij->thi", grad_half, prior_half, preferred_element_type=jnp.float32)
    )
    grad_state = jnp.einsum("thi,thj->hij", queries, grad_half, preferred_element_type=jnp.float32)
    later = chunked_scan(grad_state, True)
    later_half = later.astype(jnp.bfloat16)
    grad_k = jnp.einsum("hts,thi->shi", dscore_half, queries, preferred_element_type=jnp.float32)
    grad_k = scaling * (
        grad_k
        + jnp.einsum("shj,hij->shi", value_rows, later_half, preferred_element_type=jnp.float32)
    )
    grad_v = jnp.einsum("hts,thj->shj", score_half, grad_half, preferred_element_type=jnp.float32)
    grad_v = grad_v + scaling * jnp.einsum(
        "shi,hij->shj", key_rows, later_half, preferred_element_type=jnp.float32
    )
    width = HEADS * HEAD
    return (
        normed.astype(jnp.bfloat16),
        grad_q.reshape(rows_dev, width).astype(jnp.bfloat16),
        grad_k.reshape(rows_dev, width).astype(jnp.bfloat16),
        grad_v.reshape(rows_dev, width).astype(jnp.bfloat16),
    )


def solution(mesh):
    placed = P(("grp", "outer", "inner"), None)
    return jax.shard_map(
        per_device,
        mesh=mesh,
        in_specs=(placed, placed, placed, placed),
        out_specs=(placed, placed, placed, placed),
        check_vma=False,
    )
```

```python
import jax
import jax.numpy as jnp
from jax import lax
from jax.sharding import PartitionSpec as P

HEADS = 8
HEAD = 128


def axis_bits(axis):
    count = lax.axis_size(axis)
    return [1 << k for k in range(count.bit_length() - 1)]


def swap(value, axis, bit):
    count = lax.axis_size(axis)
    return lax.ppermute(value, axis, [(i, i ^ bit) for i in range(count)])


def partner_counts(axis, bit, backward):
    partner_lower = (lax.axis_index(axis) & bit) != 0
    return jnp.logical_not(partner_lower) if backward else partner_lower


def subcube_step(earlier, total, axis, bit, backward):
    got = swap(total, axis, bit)
    earlier = jnp.where(partner_counts(axis, bit, backward), earlier + got, earlier)
    return earlier, total + got


def scan_inner_first(value, backward):
    earlier, total = jnp.zeros_like(value), value
    for axis in ("inner", "outer"):
        for bit in axis_bits(axis):
            earlier, total = subcube_step(earlier, total, axis, bit, backward)
    return earlier


def chunked_scan(value, backward):
    half = value.shape[0] // 2
    group_a, group_b = value[:half], value[half:]
    if backward:
        group_a, group_b = group_b, group_a
    inner_bits, outer_bits = axis_bits("inner"), axis_bits("outer")
    if not inner_bits:
        return scan_inner_first(value, backward)
    earlier_a, total_a = subcube_step(
        jnp.zeros_like(group_a), group_a, "inner", inner_bits[0], backward
    )
    earlier_b, total_b = jnp.zeros_like(group_b), group_b
    for bit in inner_bits[1:]:
        earlier_b, total_b = subcube_step(earlier_b, total_b, "inner", bit, backward)
    total_b, _ = lax.optimization_barrier((total_b, total_a))
    rows_before, rows_total = jnp.zeros_like(group_b), total_b
    for index, bit in enumerate(outer_bits):
        rows_before, rows_total = subcube_step(rows_before, rows_total, "outer", bit, backward)
        if index == 0:
            total_a, _ = lax.optimization_barrier((total_a, rows_total))
    for bit in inner_bits[1:]:
        earlier_a, total_a = subcube_step(earlier_a, total_a, "inner", bit, backward)
    for bit in outer_bits:
        earlier_a, total_a = subcube_step(earlier_a, total_a, "outer", bit, backward)
    low = inner_bits[0]
    counted = partner_counts("inner", low, backward)
    known = rows_before + earlier_b
    sent = jnp.where(counted, known, known + group_b)
    earlier_b = known + swap(sent, "inner", low)
    if backward:
        earlier_a, earlier_b = earlier_b, earlier_a
    return jnp.concatenate([earlier_a, earlier_b], axis=0)


def per_device(query, key, value, grad_out):
    rows_dev = query.shape[0]
    scaling = HEAD ** (-0.5)
    queries = query.reshape(rows_dev, HEADS, HEAD)
    key_rows = key.reshape(rows_dev, HEADS, HEAD)
    value_rows = value.reshape(rows_dev, HEADS, HEAD)
    line = lax.broadcasted_iota(jnp.int32, (rows_dev, rows_dev), 0)
    column = lax.broadcasted_iota(jnp.int32, (rows_dev, rows_dev), 1)
    causal = (line >= column)[None]
    state = jnp.einsum("thi,thj->hij", key_rows, value_rows, preferred_element_type=jnp.float32)
    prior = chunked_scan(state, False)
    prior_half = prior.astype(jnp.bfloat16)
    scores = (
        jnp.einsum("thi,shi->hts", queries, key_rows, preferred_element_type=jnp.float32) * scaling
    )
    score_half = jnp.where(causal, scores, 0.0).astype(jnp.bfloat16)
    attended = jnp.einsum(
        "hts,shj->thj", score_half, value_rows, preferred_element_type=jnp.float32
    )
    attended = attended + scaling * jnp.einsum(
        "thi,hij->thj", queries, prior_half, preferred_element_type=jnp.float32
    )
    flat = attended.reshape(rows_dev, HEADS * HEAD)
    inverse = lax.rsqrt(jnp.mean(flat * flat, axis=-1, keepdims=True) + 1e-05)
    normed = flat * inverse
    grads_flat = grad_out.astype(jnp.float32)
    grad_pre = inverse * (
        grads_flat - normed * jnp.mean(grads_flat * normed, axis=-1, keepdims=True)
    )
    grad_half = grad_pre.astype(jnp.bfloat16).reshape(rows_dev, HEADS, HEAD)
    dscores = jnp.einsum("thj,shj->hts", grad_half, value_rows, preferred_element_type=jnp.float32)
    dscore_half = jnp.where(causal, dscores, 0.0).astype(jnp.bfloat16)
    grad_q = jnp.einsum("hts,shi->thi", dscore_half, key_rows, preferred_element_type=jnp.float32)
    grad_q = scaling * (
        grad_q
        + jnp.einsum("thj,hij->thi", grad_half, prior_half, preferred_element_type=jnp.float32)
    )
    grad_state = jnp.einsum("thi,thj->hij", queries, grad_half, preferred_element_type=jnp.float32)
    later = chunked_scan(grad_state, True)
    later_half = later.astype(jnp.bfloat16)
    grad_k = jnp.einsum("hts,thi->shi", dscore_half, queries, preferred_element_type=jnp.float32)
    grad_k = scaling * (
        grad_k
        + jnp.einsum("shj,hij->shi", value_rows, later_half, preferred_element_type=jnp.float32)
    )
    grad_v = jnp.einsum("hts,thj->shj", score_half, grad_half, preferred_element_type=jnp.float32)
    grad_v = grad_v + scaling * jnp.einsum(
        "shi,hij->shj", key_rows, later_half, preferred_element_type=jnp.float32
    )
    width = HEADS * HEAD
    return (
        normed.astype(jnp.bfloat16),
        grad_q.reshape(rows_dev, width).astype(jnp.bfloat16),
        grad_k.reshape(rows_dev, width).astype(jnp.bfloat16),
        grad_v.reshape(rows_dev, width).astype(jnp.bfloat16),
    )


def solution(mesh):
    placed = P(("grp", "outer", "inner"), None)
    return jax.shard_map(
        per_device,
        mesh=mesh,
        in_specs=(placed, placed, placed, placed),
        out_specs=(placed, placed, placed, placed),
        check_vma=False,
    )
```

```python
import jax
import jax.numpy as jnp
from jax import lax
from jax.sharding import PartitionSpec as P

HEADS = 8
HEAD = 128


def axis_bits(axis):
    count = lax.axis_size(axis)
    return [1 << k for k in range(count.bit_length() - 1)]


def swap(value, axis, bit):
    count = lax.axis_size(axis)
    return lax.ppermute(value, axis, [(i, i ^ bit) for i in range(count)])


def partner_counts(axis, bit, backward):
    partner_lower = (lax.axis_index(axis) & bit) != 0
    return jnp.logical_not(partner_lower) if backward else partner_lower


def subcube_step(earlier, total, axis, bit, backward):
    got = swap(total, axis, bit)
    counted = partner_counts(axis, bit, backward)
    return earlier + [jnp.where(counted, got, 0.0)], total + got


def added(pieces, like):
    total = jnp.zeros_like(like)
    for piece in pieces:
        total = total + piece
    return total


def scan_inner_first(value, backward):
    earlier, total = [], value
    for axis in ("inner", "outer"):
        for bit in axis_bits(axis):
            earlier, total = subcube_step(earlier, total, axis, bit, backward)
    return added(earlier, value)


def chunked_scan(value, backward):
    half = value.shape[0] // 2
    group_a, group_b = value[:half], value[half:]
    if backward:
        group_a, group_b = group_b, group_a
    inner_bits, outer_bits = axis_bits("inner"), axis_bits("outer")
    if not inner_bits:
        return scan_inner_first(value, backward)
    earlier_a, total_a = subcube_step([], group_a, "inner", inner_bits[0], backward)
    earlier_b, total_b = [], group_b
    for bit in inner_bits[1:]:
        earlier_b, total_b = subcube_step(earlier_b, total_b, "inner", bit, backward)
    (earlier_b, total_b), _ = lax.optimization_barrier(((earlier_b, total_b), total_a))
    rows_before, rows_total = [], total_b
    for index, bit in enumerate(outer_bits):
        rows_before, rows_total = subcube_step(rows_before, rows_total, "outer", bit, backward)
        if index == 0:
            (earlier_a, total_a), _ = lax.optimization_barrier(((earlier_a, total_a), rows_total))
    for bit in inner_bits[1:]:
        earlier_a, total_a = subcube_step(earlier_a, total_a, "inner", bit, backward)
    for bit in outer_bits:
        earlier_a, total_a = subcube_step(earlier_a, total_a, "outer", bit, backward)
    low = inner_bits[0]
    counted = partner_counts("inner", low, backward)
    known = added(rows_before + earlier_b, group_b)
    sent = jnp.where(counted, known, known + group_b)
    earlier_a = added(earlier_a, group_a)
    earlier_b = known + swap(sent, "inner", low)
    if backward:
        earlier_a, earlier_b = earlier_b, earlier_a
    return jnp.concatenate([earlier_a, earlier_b], axis=0)


def per_device(query, key, value, grad_out):
    rows_dev = query.shape[0]
    scaling = HEAD ** (-0.5)
    queries = query.reshape(rows_dev, HEADS, HEAD)
    key_rows = key.reshape(rows_dev, HEADS, HEAD)
    value_rows = value.reshape(rows_dev, HEADS, HEAD)
    line = lax.broadcasted_iota(jnp.int32, (rows_dev, rows_dev), 0)
    column = lax.broadcasted_iota(jnp.int32, (rows_dev, rows_dev), 1)
    causal = (line >= column)[None]
    state = jnp.einsum("thi,thj->hij", key_rows, value_rows, preferred_element_type=jnp.float32)
    prior = chunked_scan(state, False)
    prior_half = prior.astype(jnp.bfloat16)
    scores = (
        jnp.einsum("thi,shi->hts", queries, key_rows, preferred_element_type=jnp.float32) * scaling
    )
    score_half = jnp.where(causal, scores, 0.0).astype(jnp.bfloat16)
    attended = jnp.einsum(
        "hts,shj->thj", score_half, value_rows, preferred_element_type=jnp.float32
    )
    attended = attended + scaling * jnp.einsum(
        "thi,hij->thj", queries, prior_half, preferred_element_type=jnp.float32
    )
    flat = attended.reshape(rows_dev, HEADS * HEAD)
    inverse = lax.rsqrt(jnp.mean(flat * flat, axis=-1, keepdims=True) + 1e-05)
    normed = flat * inverse
    grads_flat = grad_out.astype(jnp.float32)
    grad_pre = inverse * (
        grads_flat - normed * jnp.mean(grads_flat * normed, axis=-1, keepdims=True)
    )
    grad_half = grad_pre.astype(jnp.bfloat16).reshape(rows_dev, HEADS, HEAD)
    dscores = jnp.einsum("thj,shj->hts", grad_half, value_rows, preferred_element_type=jnp.float32)
    dscore_half = jnp.where(causal, dscores, 0.0).astype(jnp.bfloat16)
    grad_q = jnp.einsum("hts,shi->thi", dscore_half, key_rows, preferred_element_type=jnp.float32)
    grad_q = scaling * (
        grad_q
        + jnp.einsum("thj,hij->thi", grad_half, prior_half, preferred_element_type=jnp.float32)
    )
    grad_state = jnp.einsum("thi,thj->hij", queries, grad_half, preferred_element_type=jnp.float32)
    later = chunked_scan(grad_state, True)
    later_half = later.astype(jnp.bfloat16)
    grad_k = jnp.einsum("hts,thi->shi", dscore_half, queries, preferred_element_type=jnp.float32)
    grad_k = scaling * (
        grad_k
        + jnp.einsum("shj,hij->shi", value_rows, later_half, preferred_element_type=jnp.float32)
    )
    grad_v = jnp.einsum("hts,thj->shj", score_half, grad_half, preferred_element_type=jnp.float32)
    grad_v = grad_v + scaling * jnp.einsum(
        "shi,hij->shj", key_rows, later_half, preferred_element_type=jnp.float32
    )
    width = HEADS * HEAD
    return (
        normed.astype(jnp.bfloat16),
        grad_q.reshape(rows_dev, width).astype(jnp.bfloat16),
        grad_k.reshape(rows_dev, width).astype(jnp.bfloat16),
        grad_v.reshape(rows_dev, width).astype(jnp.bfloat16),
    )


def solution(mesh):
    placed = P(("grp", "outer", "inner"), None)
    return jax.shard_map(
        per_device,
        mesh=mesh,
        in_specs=(placed, placed, placed, placed),
        out_specs=(placed, placed, placed, placed),
        check_vma=False,
    )
```

```python
import jax
import jax.numpy as jnp
from jax import lax
from jax.sharding import PartitionSpec as P

HEADS = 8
HEAD = 128


def axis_bits(axis):
    count = lax.axis_size(axis)
    return [1 << k for k in range(count.bit_length() - 1)]


def swap(value, axis, bit):
    count = lax.axis_size(axis)
    return lax.ppermute(value, axis, [(i, i ^ bit) for i in range(count)])


def partner_counts(axis, bit, backward):
    partner_lower = (lax.axis_index(axis) & bit) != 0
    return jnp.logical_not(partner_lower) if backward else partner_lower


def subcube_step(earlier, total, axis, bit, backward):
    got = swap(total, axis, bit)
    counted = partner_counts(axis, bit, backward)
    return earlier + [jnp.where(counted, got, 0.0)], total + got


def after(value, other):
    return value + 0.0 * other[:1, :1, :1]


def added(pieces, like):
    total = jnp.zeros_like(like)
    for piece in pieces:
        total = total + piece
    return total


def scan_inner_first(value, backward):
    earlier, total = [], value
    for axis in ("inner", "outer"):
        for bit in axis_bits(axis):
            earlier, total = subcube_step(earlier, total, axis, bit, backward)
    return added(earlier, value)


def chunked_scan(value, backward):
    half = value.shape[0] // 2
    group_a, group_b = value[:half], value[half:]
    if backward:
        group_a, group_b = group_b, group_a
    inner_bits, outer_bits = axis_bits("inner"), axis_bits("outer")
    if not inner_bits:
        return scan_inner_first(value, backward)
    earlier_a, total_a = subcube_step([], group_a, "inner", inner_bits[0], backward)
    earlier_b, total_b = [], group_b
    for bit in inner_bits[1:]:
        earlier_b, total_b = subcube_step(earlier_b, total_b, "inner", bit, backward)
    (earlier_b, total_b), _ = lax.optimization_barrier(((earlier_b, total_b), total_a))
    rows_before, rows_total = [], total_b
    for index, bit in enumerate(outer_bits):
        rows_before, rows_total = subcube_step(rows_before, rows_total, "outer", bit, backward)
        if index == 0:
            total_a = after(total_a, rows_total)
    for bit in inner_bits[1:]:
        earlier_a, total_a = subcube_step(earlier_a, total_a, "inner", bit, backward)
    for bit in outer_bits:
        earlier_a, total_a = subcube_step(earlier_a, total_a, "outer", bit, backward)
    low = inner_bits[0]
    counted = partner_counts("inner", low, backward)
    known = added(rows_before + earlier_b, group_b)
    sent = jnp.where(counted, known, known + group_b)
    earlier_a = added(earlier_a, group_a)
    earlier_b = known + swap(sent, "inner", low)
    if backward:
        earlier_a, earlier_b = earlier_b, earlier_a
    return jnp.concatenate([earlier_a, earlier_b], axis=0)


def per_device(query, key, value, grad_out):
    rows_dev = query.shape[0]
    scaling = HEAD ** (-0.5)
    queries = query.reshape(rows_dev, HEADS, HEAD)
    key_rows = key.reshape(rows_dev, HEADS, HEAD)
    value_rows = value.reshape(rows_dev, HEADS, HEAD)
    line = lax.broadcasted_iota(jnp.int32, (rows_dev, rows_dev), 0)
    column = lax.broadcasted_iota(jnp.int32, (rows_dev, rows_dev), 1)
    causal = (line >= column)[None]
    state = jnp.einsum("thi,thj->hij", key_rows, value_rows, preferred_element_type=jnp.float32)
    prior = chunked_scan(state, False)
    prior_half = prior.astype(jnp.bfloat16)
    scores = (
        jnp.einsum("thi,shi->hts", queries, key_rows, preferred_element_type=jnp.float32) * scaling
    )
    score_half = jnp.where(causal, scores, 0.0).astype(jnp.bfloat16)
    attended = jnp.einsum(
        "hts,shj->thj", score_half, value_rows, preferred_element_type=jnp.float32
    )
    attended = attended + scaling * jnp.einsum(
        "thi,hij->thj", queries, prior_half, preferred_element_type=jnp.float32
    )
    flat = attended.reshape(rows_dev, HEADS * HEAD)
    inverse = lax.rsqrt(jnp.mean(flat * flat, axis=-1, keepdims=True) + 1e-05)
    normed = flat * inverse
    grads_flat = grad_out.astype(jnp.float32)
    grad_pre = inverse * (
        grads_flat - normed * jnp.mean(grads_flat * normed, axis=-1, keepdims=True)
    )
    grad_half = grad_pre.astype(jnp.bfloat16).reshape(rows_dev, HEADS, HEAD)
    dscores = jnp.einsum("thj,shj->hts", grad_half, value_rows, preferred_element_type=jnp.float32)
    dscore_half = jnp.where(causal, dscores, 0.0).astype(jnp.bfloat16)
    grad_q = jnp.einsum("hts,shi->thi", dscore_half, key_rows, preferred_element_type=jnp.float32)
    grad_q = scaling * (
        grad_q
        + jnp.einsum("thj,hij->thi", grad_half, prior_half, preferred_element_type=jnp.float32)
    )
    grad_state = jnp.einsum("thi,thj->hij", queries, grad_half, preferred_element_type=jnp.float32)
    later = chunked_scan(grad_state, True)
    later_half = later.astype(jnp.bfloat16)
    grad_k = jnp.einsum("hts,thi->shi", dscore_half, queries, preferred_element_type=jnp.float32)
    grad_k = scaling * (
        grad_k
        + jnp.einsum("shj,hij->shi", value_rows, later_half, preferred_element_type=jnp.float32)
    )
    grad_v = jnp.einsum("hts,thj->shj", score_half, grad_half, preferred_element_type=jnp.float32)
    grad_v = grad_v + scaling * jnp.einsum(
        "shi,hij->shj", key_rows, later_half, preferred_element_type=jnp.float32
    )
    width = HEADS * HEAD
    return (
        normed.astype(jnp.bfloat16),
        grad_q.reshape(rows_dev, width).astype(jnp.bfloat16),
        grad_k.reshape(rows_dev, width).astype(jnp.bfloat16),
        grad_v.reshape(rows_dev, width).astype(jnp.bfloat16),
    )


def solution(mesh):
    placed = P(("grp", "outer", "inner"), None)
    return jax.shard_map(
        per_device,
        mesh=mesh,
        in_specs=(placed, placed, placed, placed),
        out_specs=(placed, placed, placed, placed),
        check_vma=False,
    )
```

```python
import jax
import jax.numpy as jnp
from jax import lax
from jax.sharding import PartitionSpec as P

HEADS = 8
HEAD = 128


def axis_bits(axis):
    count = lax.axis_size(axis)
    return [1 << k for k in range(count.bit_length() - 1)]


def swap(value, axis, bit):
    count = lax.axis_size(axis)
    return lax.ppermute(value, axis, [(i, i ^ bit) for i in range(count)])


def partner_counts(axis, bit, backward):
    partner_lower = (lax.axis_index(axis) & bit) != 0
    return jnp.logical_not(partner_lower) if backward else partner_lower


def subcube_step(earlier, total, axis, bit, backward):
    got = swap(total, axis, bit)
    counted = partner_counts(axis, bit, backward)
    return earlier + [jnp.where(counted, got, 0.0)], total + got


def added(pieces, like):
    total = jnp.zeros_like(like)
    for piece in pieces:
        total = total + piece
    return total


def scan_inner_first(value, backward):
    earlier, total = [], value
    for axis in ("inner", "outer"):
        for bit in axis_bits(axis):
            earlier, total = subcube_step(earlier, total, axis, bit, backward)
    return added(earlier, value)


def chunked_scan(value, backward):
    half = value.shape[0] // 2
    group_a, group_b = value[:half], value[half:]
    if backward:
        group_a, group_b = group_b, group_a
    inner_bits, outer_bits = axis_bits("inner"), axis_bits("outer")
    if not inner_bits:
        return scan_inner_first(value, backward)
    earlier_a, total_a = subcube_step([], group_a, "inner", inner_bits[0], backward)
    earlier_b, total_b = [], group_b
    for bit in inner_bits[1:]:
        earlier_b, total_b = subcube_step(earlier_b, total_b, "inner", bit, backward)
    (earlier_b, total_b), _ = lax.optimization_barrier(((earlier_b, total_b), total_a))
    rows_before, rows_total = [], total_b
    for index, bit in enumerate(outer_bits):
        rows_before, rows_total = subcube_step(rows_before, rows_total, "outer", bit, backward)
        if index == 0 and not backward:
            (earlier_a, total_a), _ = lax.optimization_barrier(((earlier_a, total_a), rows_total))
    for bit in inner_bits[1:]:
        earlier_a, total_a = subcube_step(earlier_a, total_a, "inner", bit, backward)
    for bit in outer_bits:
        earlier_a, total_a = subcube_step(earlier_a, total_a, "outer", bit, backward)
    low = inner_bits[0]
    counted = partner_counts("inner", low, backward)
    known = added(rows_before + earlier_b, group_b)
    sent = jnp.where(counted, known, known + group_b)
    earlier_a = added(earlier_a, group_a)
    earlier_b = known + swap(sent, "inner", low)
    if backward:
        earlier_a, earlier_b = earlier_b, earlier_a
    return jnp.concatenate([earlier_a, earlier_b], axis=0)


def per_device(query, key, value, grad_out):
    rows_dev = query.shape[0]
    scaling = HEAD ** (-0.5)
    queries = query.reshape(rows_dev, HEADS, HEAD)
    key_rows = key.reshape(rows_dev, HEADS, HEAD)
    value_rows = value.reshape(rows_dev, HEADS, HEAD)
    line = lax.broadcasted_iota(jnp.int32, (rows_dev, rows_dev), 0)
    column = lax.broadcasted_iota(jnp.int32, (rows_dev, rows_dev), 1)
    causal = (line >= column)[None]
    state = jnp.einsum("thi,thj->hij", key_rows, value_rows, preferred_element_type=jnp.float32)
    prior = chunked_scan(state, False)
    prior_half = prior.astype(jnp.bfloat16)
    scores = (
        jnp.einsum("thi,shi->hts", queries, key_rows, preferred_element_type=jnp.float32) * scaling
    )
    score_half = jnp.where(causal, scores, 0.0).astype(jnp.bfloat16)
    attended = jnp.einsum(
        "hts,shj->thj", score_half, value_rows, preferred_element_type=jnp.float32
    )
    attended = attended + scaling * jnp.einsum(
        "thi,hij->thj", queries, prior_half, preferred_element_type=jnp.float32
    )
    flat = attended.reshape(rows_dev, HEADS * HEAD)
    inverse = lax.rsqrt(jnp.mean(flat * flat, axis=-1, keepdims=True) + 1e-05)
    normed = flat * inverse
    grads_flat = grad_out.astype(jnp.float32)
    grad_pre = inverse * (
        grads_flat - normed * jnp.mean(grads_flat * normed, axis=-1, keepdims=True)
    )
    grad_half = grad_pre.astype(jnp.bfloat16).reshape(rows_dev, HEADS, HEAD)
    dscores = jnp.einsum("thj,shj->hts", grad_half, value_rows, preferred_element_type=jnp.float32)
    dscore_half = jnp.where(causal, dscores, 0.0).astype(jnp.bfloat16)
    grad_q = jnp.einsum("hts,shi->thi", dscore_half, key_rows, preferred_element_type=jnp.float32)
    grad_q = scaling * (
        grad_q
        + jnp.einsum("thj,hij->thi", grad_half, prior_half, preferred_element_type=jnp.float32)
    )
    grad_state = jnp.einsum("thi,thj->hij", queries, grad_half, preferred_element_type=jnp.float32)
    later = chunked_scan(grad_state, True)
    later_half = later.astype(jnp.bfloat16)
    grad_k = jnp.einsum("hts,thi->shi", dscore_half, queries, preferred_element_type=jnp.float32)
    grad_k = scaling * (
        grad_k
        + jnp.einsum("shj,hij->shi", value_rows, later_half, preferred_element_type=jnp.float32)
    )
    grad_v = jnp.einsum("hts,thj->shj", score_half, grad_half, preferred_element_type=jnp.float32)
    grad_v = grad_v + scaling * jnp.einsum(
        "shi,hij->shj", key_rows, later_half, preferred_element_type=jnp.float32
    )
    width = HEADS * HEAD
    return (
        normed.astype(jnp.bfloat16),
        grad_q.reshape(rows_dev, width).astype(jnp.bfloat16),
        grad_k.reshape(rows_dev, width).astype(jnp.bfloat16),
        grad_v.reshape(rows_dev, width).astype(jnp.bfloat16),
    )


def solution(mesh):
    placed = P(("grp", "outer", "inner"), None)
    return jax.shard_map(
        per_device,
        mesh=mesh,
        in_specs=(placed, placed, placed, placed),
        out_specs=(placed, placed, placed, placed),
        check_vma=False,
    )
```

```python
import jax
import jax.numpy as jnp
from jax import lax
from jax.sharding import PartitionSpec as P

HEADS = 8
HEAD = 128


def axis_bits(axis):
    count = lax.axis_size(axis)
    return [1 << k for k in range(count.bit_length() - 1)]


def swap(value, axis, bit):
    count = lax.axis_size(axis)
    return lax.ppermute(value, axis, [(i, i ^ bit) for i in range(count)])


def partner_counts(axis, bit, backward):
    partner_lower = (lax.axis_index(axis) & bit) != 0
    return jnp.logical_not(partner_lower) if backward else partner_lower


def subcube_step(earlier, total, axis, bit, backward):
    got = swap(total, axis, bit)
    counted = partner_counts(axis, bit, backward)
    return earlier + [jnp.where(counted, got, 0.0)], total + got


def added(pieces, like):
    total = jnp.zeros_like(like)
    for piece in pieces:
        total = total + piece
    return total


def scan_inner_first(value, backward):
    earlier, total = [], value
    for axis in ("inner", "outer"):
        for bit in axis_bits(axis):
            earlier, total = subcube_step(earlier, total, axis, bit, backward)
    return added(earlier, value)


def chunked_scan(value, backward):
    half = value.shape[0] // 2
    group_a, group_b = value[:half], value[half:]
    if backward:
        group_a, group_b = group_b, group_a
    inner_bits, outer_bits = axis_bits("inner"), axis_bits("outer")
    if not inner_bits:
        return scan_inner_first(value, backward)
    earlier_a, total_a = subcube_step([], group_a, "inner", inner_bits[0], backward)
    earlier_b, total_b = [], group_b
    for bit in inner_bits[1:]:
        earlier_b, total_b = subcube_step(earlier_b, total_b, "inner", bit, backward)
    (earlier_b, total_b), _ = lax.optimization_barrier(((earlier_b, total_b), total_a))
    rows_before, rows_total = [], total_b
    for index, bit in enumerate(outer_bits):
        rows_before, rows_total = subcube_step(rows_before, rows_total, "outer", bit, backward)
        if index == 0 and not backward:
            (earlier_a, total_a), _ = lax.optimization_barrier(((earlier_a, total_a), rows_total))
    for bit in inner_bits[1:]:
        earlier_a, total_a = subcube_step(earlier_a, total_a, "inner", bit, backward)
    for bit in outer_bits:
        earlier_a, total_a = subcube_step(earlier_a, total_a, "outer", bit, backward)
    low = inner_bits[0]
    counted = partner_counts("inner", low, backward)
    known = added(rows_before + earlier_b, group_b)
    sent = jnp.where(counted, known, known + group_b)
    earlier_a = added(earlier_a, group_a)
    earlier_b = known + swap(sent, "inner", low)
    if backward:
        earlier_a, earlier_b = earlier_b, earlier_a
    return earlier_a, earlier_b


def per_device(query, key, value, grad_out):
    rows_dev = query.shape[0]
    scaling = HEAD ** (-0.5)
    queries = query.reshape(rows_dev, HEADS, HEAD)
    key_rows = key.reshape(rows_dev, HEADS, HEAD)
    value_rows = value.reshape(rows_dev, HEADS, HEAD)
    line = lax.broadcasted_iota(jnp.int32, (rows_dev, rows_dev), 0)
    column = lax.broadcasted_iota(jnp.int32, (rows_dev, rows_dev), 1)
    causal = (line >= column)[None]
    state = jnp.einsum("thi,thj->hij", key_rows, value_rows, preferred_element_type=jnp.float32)
    prior = jnp.concatenate(chunked_scan(state, False), axis=0)
    prior_half = prior.astype(jnp.bfloat16)
    scores = (
        jnp.einsum("thi,shi->hts", queries, key_rows, preferred_element_type=jnp.float32) * scaling
    )
    score_half = jnp.where(causal, scores, 0.0).astype(jnp.bfloat16)
    attended = jnp.einsum(
        "hts,shj->thj", score_half, value_rows, preferred_element_type=jnp.float32
    )
    attended = attended + scaling * jnp.einsum(
        "thi,hij->thj", queries, prior_half, preferred_element_type=jnp.float32
    )
    flat = attended.reshape(rows_dev, HEADS * HEAD)
    inverse = lax.rsqrt(jnp.mean(flat * flat, axis=-1, keepdims=True) + 1e-05)
    normed = flat * inverse
    grads_flat = grad_out.astype(jnp.float32)
    grad_pre = inverse * (
        grads_flat - normed * jnp.mean(grads_flat * normed, axis=-1, keepdims=True)
    )
    grad_half = grad_pre.astype(jnp.bfloat16).reshape(rows_dev, HEADS, HEAD)
    dscores = jnp.einsum("thj,shj->hts", grad_half, value_rows, preferred_element_type=jnp.float32)
    dscore_half = jnp.where(causal, dscores, 0.0).astype(jnp.bfloat16)
    grad_q = jnp.einsum("hts,shi->thi", dscore_half, key_rows, preferred_element_type=jnp.float32)
    grad_q = scaling * (
        grad_q
        + jnp.einsum("thj,hij->thi", grad_half, prior_half, preferred_element_type=jnp.float32)
    )
    grad_state = jnp.einsum("thi,thj->hij", queries, grad_half, preferred_element_type=jnp.float32)
    half = HEADS // 2
    grad_k, grad_v = [], []
    for heads, later in zip((slice(0, half), slice(half, HEADS)), chunked_scan(grad_state, True)):
        later_half = later.astype(jnp.bfloat16)
        queries_part, key_part, value_part = queries[:, heads], key_rows[:, heads], value_rows[:, heads]
        part_k = jnp.einsum(
            "hts,thi->shi", dscore_half[heads], queries_part, preferred_element_type=jnp.float32
        )
        grad_k.append(
            scaling
            * (
                part_k
                + jnp.einsum(
                    "shj,hij->shi", value_part, later_half, preferred_element_type=jnp.float32
                )
            )
        )
        part_v = jnp.einsum(
            "hts,thj->shj", score_half[heads], grad_half[:, heads], preferred_element_type=jnp.float32
        )
        grad_v.append(
            part_v
            + scaling
            * jnp.einsum("shi,hij->shj", key_part, later_half, preferred_element_type=jnp.float32)
        )
    grad_k = jnp.concatenate(grad_k, axis=1)
    grad_v = jnp.concatenate(grad_v, axis=1)
    width = HEADS * HEAD
    return (
        normed.astype(jnp.bfloat16),
        grad_q.reshape(rows_dev, width).astype(jnp.bfloat16),
        grad_k.reshape(rows_dev, width).astype(jnp.bfloat16),
        grad_v.reshape(rows_dev, width).astype(jnp.bfloat16),
    )


def solution(mesh):
    placed = P(("grp", "outer", "inner"), None)
    return jax.shard_map(
        per_device,
        mesh=mesh,
        in_specs=(placed, placed, placed, placed),
        out_specs=(placed, placed, placed, placed),
        check_vma=False,
    )
```

```python
import functools

import jax
import jax.numpy as jnp
from jax import lax
from jax.experimental import pallas as pl
from jax.experimental.pallas import tpu as pltpu
from jax.sharding import PartitionSpec as P

HEADS = 8
HEAD = 128


def axis_bits(axis):
    count = lax.axis_size(axis)
    return [1 << k for k in range(count.bit_length() - 1)]


def swap(value, axis, bit):
    count = lax.axis_size(axis)
    return lax.ppermute(value, axis, [(i, i ^ bit) for i in range(count)])


def partner_counts(axis, bit, backward):
    partner_lower = (lax.axis_index(axis) & bit) != 0
    return jnp.logical_not(partner_lower) if backward else partner_lower


def subcube_step(earlier, total, axis, bit, backward):
    got = swap(total, axis, bit)
    counted = partner_counts(axis, bit, backward)
    return earlier + [jnp.where(counted, got, 0.0)], total + got


def added(pieces, like):
    total = jnp.zeros_like(like)
    for piece in pieces:
        total = total + piece
    return total


def scan_inner_first(value, backward):
    earlier, total = [], value
    for axis in ("inner", "outer"):
        for bit in axis_bits(axis):
            earlier, total = subcube_step(earlier, total, axis, bit, backward)
    return added(earlier, value)


def chunked_scan(value, backward):
    half = value.shape[0] // 2
    group_a, group_b = value[:half], value[half:]
    if backward:
        group_a, group_b = group_b, group_a
    inner_bits, outer_bits = axis_bits("inner"), axis_bits("outer")
    if not inner_bits:
        result = scan_inner_first(value, backward)
        if backward:
            return result[:half], jnp.zeros_like(result[:half]), result[half:]
        return result
    earlier_a, total_a = subcube_step([], group_a, "inner", inner_bits[0], backward)
    earlier_b, total_b = [], group_b
    for bit in inner_bits[1:]:
        earlier_b, total_b = subcube_step(earlier_b, total_b, "inner", bit, backward)
    (earlier_b, total_b), _ = lax.optimization_barrier(((earlier_b, total_b), total_a))
    rows_before, rows_total = [], total_b
    for index, bit in enumerate(outer_bits):
        rows_before, rows_total = subcube_step(rows_before, rows_total, "outer", bit, backward)
        if index == 0 and not backward:
            (earlier_a, total_a), _ = lax.optimization_barrier(((earlier_a, total_a), rows_total))
    for bit in inner_bits[1:]:
        earlier_a, total_a = subcube_step(earlier_a, total_a, "inner", bit, backward)
    for bit in outer_bits:
        earlier_a, total_a = subcube_step(earlier_a, total_a, "outer", bit, backward)
    low = inner_bits[0]
    counted = partner_counts("inner", low, backward)
    known = added(rows_before + earlier_b, group_b)
    sent = jnp.where(counted, known, known + group_b)
    earlier_a = added(earlier_a, group_a)
    got_b = swap(sent, "inner", low)
    if backward:
        return known, got_b, earlier_a
    return jnp.concatenate([earlier_a, known + got_b], axis=0)


def tail_kernel(
    scaling, lower_known, lower_got, upper_later, local_k, local_v, value, key, out_k, out_v
):
    half = HEADS // 2
    for h in range(HEADS):
        later = lower_known[h] + lower_got[h] if h < half else upper_later[h - half]
        later_half = later.astype(jnp.bfloat16)
        cols = slice(h * HEAD, (h + 1) * HEAD)
        from_later_k = lax.dot_general(
            value[:, cols], later_half, (((1,), (1,)), ((), ())), preferred_element_type=jnp.float32
        )
        out_k[:, cols] = (scaling * (local_k[h] + from_later_k)).astype(out_k.dtype)
        from_later_v = lax.dot_general(
            key[:, cols], later_half, (((1,), (0,)), ((), ())), preferred_element_type=jnp.float32
        )
        out_v[:, cols] = (local_v[h] + scaling * from_later_v).astype(out_v.dtype)


def tail(lower_known, lower_got, upper_later, local_k, local_v, value, key):
    rows = value.shape[0]
    vmem = pl.BlockSpec(memory_space=pltpu.VMEM)
    out = jax.ShapeDtypeStruct((rows, HEADS * HEAD), jnp.bfloat16)
    return pl.pallas_call(
        functools.partial(tail_kernel, HEAD ** (-0.5)),
        out_shape=(out, out),
        in_specs=[vmem] * 7,
        out_specs=(vmem, vmem),
        cost_estimate=pl.CostEstimate(
            flops=4 * HEADS * rows * HEAD * HEAD, transcendentals=0, bytes_accessed=12 * rows * 1024 * 4
        ),
    )(lower_known, lower_got, upper_later, local_k, local_v, value, key)


def per_device(query, key, value, grad_out):
    rows_dev = query.shape[0]
    scaling = HEAD ** (-0.5)
    queries = query.reshape(rows_dev, HEADS, HEAD)
    key_rows = key.reshape(rows_dev, HEADS, HEAD)
    value_rows = value.reshape(rows_dev, HEADS, HEAD)
    line = lax.broadcasted_iota(jnp.int32, (rows_dev, rows_dev), 0)
    column = lax.broadcasted_iota(jnp.int32, (rows_dev, rows_dev), 1)
    causal = (line >= column)[None]
    state = jnp.einsum("thi,thj->hij", key_rows, value_rows, preferred_element_type=jnp.float32)
    prior = chunked_scan(state, False)
    prior_half = prior.astype(jnp.bfloat16)
    scores = (
        jnp.einsum("thi,shi->hts", queries, key_rows, preferred_element_type=jnp.float32) * scaling
    )
    score_half = jnp.where(causal, scores, 0.0).astype(jnp.bfloat16)
    attended = jnp.einsum(
        "hts,shj->thj", score_half, value_rows, preferred_element_type=jnp.float32
    )
    attended = attended + scaling * jnp.einsum(
        "thi,hij->thj", queries, prior_half, preferred_element_type=jnp.float32
    )
    flat = attended.reshape(rows_dev, HEADS * HEAD)
    inverse = lax.rsqrt(jnp.mean(flat * flat, axis=-1, keepdims=True) + 1e-05)
    normed = flat * inverse
    grads_flat = grad_out.astype(jnp.float32)
    grad_pre = inverse * (
        grads_flat - normed * jnp.mean(grads_flat * normed, axis=-1, keepdims=True)
    )
    grad_half = grad_pre.astype(jnp.bfloat16).reshape(rows_dev, HEADS, HEAD)
    dscores = jnp.einsum("thj,shj->hts", grad_half, value_rows, preferred_element_type=jnp.float32)
    dscore_half = jnp.where(causal, dscores, 0.0).astype(jnp.bfloat16)
    grad_q = jnp.einsum("hts,shi->thi", dscore_half, key_rows, preferred_element_type=jnp.float32)
    grad_q = scaling * (
        grad_q
        + jnp.einsum("thj,hij->thi", grad_half, prior_half, preferred_element_type=jnp.float32)
    )
    grad_state = jnp.einsum("thi,thj->hij", queries, grad_half, preferred_element_type=jnp.float32)
    lower_known, lower_got, upper_later = chunked_scan(grad_state, True)
    local_k = jnp.einsum("hts,thi->hsi", dscore_half, queries, preferred_element_type=jnp.float32)
    local_v = jnp.einsum("hts,thj->hsj", score_half, grad_half, preferred_element_type=jnp.float32)
    grad_k, grad_v = tail(lower_known, lower_got, upper_later, local_k, local_v, value, key)
    width = HEADS * HEAD
    return (
        normed.astype(jnp.bfloat16),
        grad_q.reshape(rows_dev, width).astype(jnp.bfloat16),
        grad_k,
        grad_v,
    )


def solution(mesh):
    placed = P(("grp", "outer", "inner"), None)
    return jax.shard_map(
        per_device,
        mesh=mesh,
        in_specs=(placed, placed, placed, placed),
        out_specs=(placed, placed, placed, placed),
        check_vma=False,
    )
```

```python
import functools

import jax
import jax.numpy as jnp
from jax import lax
from jax.experimental import pallas as pl
from jax.experimental.pallas import tpu as pltpu
from jax.sharding import PartitionSpec as P

HEADS = 8
HEAD = 128


def axis_bits(axis):
    count = lax.axis_size(axis)
    return [1 << k for k in range(count.bit_length() - 1)]


def swap(value, axis, bit):
    count = lax.axis_size(axis)
    return lax.ppermute(value, axis, [(i, i ^ bit) for i in range(count)])


def partner_counts(axis, bit, backward):
    partner_lower = (lax.axis_index(axis) & bit) != 0
    return jnp.logical_not(partner_lower) if backward else partner_lower


def subcube_step(earlier, total, axis, bit, backward):
    got = swap(total, axis, bit)
    counted = partner_counts(axis, bit, backward)
    return earlier + [jnp.where(counted, got, 0.0)], total + got


def added(pieces, like):
    total = jnp.zeros_like(like)
    for piece in pieces:
        total = total + piece
    return total


def scan_inner_first(value, backward):
    earlier, total = [], value
    for axis in ("inner", "outer"):
        for bit in axis_bits(axis):
            earlier, total = subcube_step(earlier, total, axis, bit, backward)
    return added(earlier, value)


def chunked_scan(value, backward):
    half = value.shape[0] // 2
    group_a, group_b = value[:half], value[half:]
    if backward:
        group_a, group_b = group_b, group_a
    inner_bits, outer_bits = axis_bits("inner"), axis_bits("outer")
    if not inner_bits:
        result = scan_inner_first(value, backward)
        if backward:
            return result[:half], jnp.zeros_like(result[:half]), result[half:]
        return result
    earlier_a, total_a = subcube_step([], group_a, "inner", inner_bits[0], backward)
    earlier_b, total_b = [], group_b
    for bit in inner_bits[1:]:
        earlier_b, total_b = subcube_step(earlier_b, total_b, "inner", bit, backward)
    (earlier_b, total_b), _ = lax.optimization_barrier(((earlier_b, total_b), total_a))
    rows_before, rows_total = [], total_b
    for index, bit in enumerate(outer_bits):
        rows_before, rows_total = subcube_step(rows_before, rows_total, "outer", bit, backward)
        if index == 0 and not backward:
            (earlier_a, total_a), _ = lax.optimization_barrier(((earlier_a, total_a), rows_total))
    for bit in inner_bits[1:]:
        earlier_a, total_a = subcube_step(earlier_a, total_a, "inner", bit, backward)
    for bit in outer_bits:
        earlier_a, total_a = subcube_step(earlier_a, total_a, "outer", bit, backward)
    low = inner_bits[0]
    counted = partner_counts("inner", low, backward)
    known = added(rows_before + earlier_b, group_b)
    sent = jnp.where(counted, known, known + group_b)
    earlier_a = added(earlier_a, group_a)
    got_b = swap(sent, "inner", low)
    if backward:
        return known, got_b, earlier_a
    return jnp.concatenate([earlier_a, known + got_b], axis=0)


def tail_kernel(scaling, *refs):
    sources, (out_k, out_v), held, semaphores = refs[:7], refs[7:9], refs[9:16], refs[16]
    copies = [
        pltpu.make_async_copy(source, target, semaphores.at[i])
        for i, (source, target) in enumerate(zip(sources, held))
    ]
    for copy in copies:
        copy.start()
    for copy in copies:
        copy.wait()
    lower_known, lower_got, upper_later, local_k, local_v, value, key = held
    half = HEADS // 2
    for h in range(HEADS):
        later = lower_known[h] + lower_got[h] if h < half else upper_later[h - half]
        later_half = later.astype(jnp.bfloat16)
        cols = slice(h * HEAD, (h + 1) * HEAD)
        from_later_k = lax.dot_general(
            value[:, cols], later_half, (((1,), (1,)), ((), ())), preferred_element_type=jnp.float32
        )
        out_k[:, cols] = (scaling * (local_k[h] + from_later_k)).astype(out_k.dtype)
        from_later_v = lax.dot_general(
            key[:, cols], later_half, (((1,), (0,)), ((), ())), preferred_element_type=jnp.float32
        )
        out_v[:, cols] = (local_v[h] + scaling * from_later_v).astype(out_v.dtype)


def tail(*operands):
    rows = operands[-1].shape[0]
    vmem = pl.BlockSpec(memory_space=pltpu.VMEM)
    anywhere = pl.BlockSpec(memory_space=pl.ANY)
    out = jax.ShapeDtypeStruct((rows, HEADS * HEAD), jnp.bfloat16)
    return pl.pallas_call(
        functools.partial(tail_kernel, HEAD ** (-0.5)),
        out_shape=(out, out),
        in_specs=[anywhere] * len(operands),
        out_specs=(vmem, vmem),
        scratch_shapes=[pltpu.VMEM(x.shape, x.dtype) for x in operands]
        + [pltpu.SemaphoreType.DMA((len(operands),))],
        cost_estimate=pl.CostEstimate(
            flops=4 * HEADS * rows * HEAD * HEAD, transcendentals=0, bytes_accessed=12 * rows * 1024 * 4
        ),
    )(*operands)


def per_device(query, key, value, grad_out):
    rows_dev = query.shape[0]
    scaling = HEAD ** (-0.5)
    queries = query.reshape(rows_dev, HEADS, HEAD)
    key_rows = key.reshape(rows_dev, HEADS, HEAD)
    value_rows = value.reshape(rows_dev, HEADS, HEAD)
    line = lax.broadcasted_iota(jnp.int32, (rows_dev, rows_dev), 0)
    column = lax.broadcasted_iota(jnp.int32, (rows_dev, rows_dev), 1)
    causal = (line >= column)[None]
    state = jnp.einsum("thi,thj->hij", key_rows, value_rows, preferred_element_type=jnp.float32)
    prior = chunked_scan(state, False)
    prior_half = prior.astype(jnp.bfloat16)
    scores = (
        jnp.einsum("thi,shi->hts", queries, key_rows, preferred_element_type=jnp.float32) * scaling
    )
    score_half = jnp.where(causal, scores, 0.0).astype(jnp.bfloat16)
    attended = jnp.einsum(
        "hts,shj->thj", score_half, value_rows, preferred_element_type=jnp.float32
    )
    attended = attended + scaling * jnp.einsum(
        "thi,hij->thj", queries, prior_half, preferred_element_type=jnp.float32
    )
    flat = attended.reshape(rows_dev, HEADS * HEAD)
    inverse = lax.rsqrt(jnp.mean(flat * flat, axis=-1, keepdims=True) + 1e-05)
    normed = flat * inverse
    grads_flat = grad_out.astype(jnp.float32)
    grad_pre = inverse * (
        grads_flat - normed * jnp.mean(grads_flat * normed, axis=-1, keepdims=True)
    )
    grad_half = grad_pre.astype(jnp.bfloat16).reshape(rows_dev, HEADS, HEAD)
    dscores = jnp.einsum("thj,shj->hts", grad_half, value_rows, preferred_element_type=jnp.float32)
    dscore_half = jnp.where(causal, dscores, 0.0).astype(jnp.bfloat16)
    grad_q = jnp.einsum("hts,shi->thi", dscore_half, key_rows, preferred_element_type=jnp.float32)
    grad_q = scaling * (
        grad_q
        + jnp.einsum("thj,hij->thi", grad_half, prior_half, preferred_element_type=jnp.float32)
    )
    grad_state = jnp.einsum("thi,thj->hij", queries, grad_half, preferred_element_type=jnp.float32)
    lower_known, lower_got, upper_later = chunked_scan(grad_state, True)
    local_k = jnp.einsum("hts,thi->hsi", dscore_half, queries, preferred_element_type=jnp.float32)
    local_v = jnp.einsum("hts,thj->hsj", score_half, grad_half, preferred_element_type=jnp.float32)
    grad_k, grad_v = tail(lower_known, lower_got, upper_later, local_k, local_v, value, key)
    width = HEADS * HEAD
    return (
        normed.astype(jnp.bfloat16),
        grad_q.reshape(rows_dev, width).astype(jnp.bfloat16),
        grad_k,
        grad_v,
    )


def solution(mesh):
    placed = P(("grp", "outer", "inner"), None)
    return jax.shard_map(
        per_device,
        mesh=mesh,
        in_specs=(placed, placed, placed, placed),
        out_specs=(placed, placed, placed, placed),
        check_vma=False,
    )
```

```python
import functools

import jax
import jax.numpy as jnp
from jax import lax
from jax.experimental import pallas as pl
from jax.experimental.pallas import tpu as pltpu
from jax.sharding import PartitionSpec as P

HEADS = 8
HEAD = 128


def axis_bits(axis):
    count = lax.axis_size(axis)
    return [1 << k for k in range(count.bit_length() - 1)]


def swap(value, axis, bit):
    count = lax.axis_size(axis)
    return lax.ppermute(value, axis, [(i, i ^ bit) for i in range(count)])


def partner_counts(axis, bit, backward):
    partner_lower = (lax.axis_index(axis) & bit) != 0
    return jnp.logical_not(partner_lower) if backward else partner_lower


def subcube_step(earlier, total, axis, bit, backward):
    got = swap(total, axis, bit)
    counted = partner_counts(axis, bit, backward)
    return earlier + [jnp.where(counted, got, 0.0)], total + got


def added(pieces, like):
    total = jnp.zeros_like(like)
    for piece in pieces:
        total = total + piece
    return total


def scan_inner_first(value, backward):
    earlier, total = [], value
    for axis in ("inner", "outer"):
        for bit in axis_bits(axis):
            earlier, total = subcube_step(earlier, total, axis, bit, backward)
    return added(earlier, value)


def chunked_scan(value, backward):
    half = value.shape[0] // 2
    group_a, group_b = value[:half], value[half:]
    if backward:
        group_a, group_b = group_b, group_a
    inner_bits, outer_bits = axis_bits("inner"), axis_bits("outer")
    if not inner_bits:
        result = scan_inner_first(value, backward)
        if backward:
            return result[:half], jnp.zeros_like(result[:half]), result[half:]
        return result
    earlier_a, total_a = subcube_step([], group_a, "inner", inner_bits[0], backward)
    earlier_b, total_b = [], group_b
    for bit in inner_bits[1:]:
        earlier_b, total_b = subcube_step(earlier_b, total_b, "inner", bit, backward)
    (earlier_b, total_b), _ = lax.optimization_barrier(((earlier_b, total_b), total_a))
    rows_before, rows_total = [], total_b
    for index, bit in enumerate(outer_bits):
        rows_before, rows_total = subcube_step(rows_before, rows_total, "outer", bit, backward)
        if index == 0 and not backward:
            (earlier_a, total_a), _ = lax.optimization_barrier(((earlier_a, total_a), rows_total))
    for bit in inner_bits[1:]:
        earlier_a, total_a = subcube_step(earlier_a, total_a, "inner", bit, backward)
    for bit in outer_bits:
        earlier_a, total_a = subcube_step(earlier_a, total_a, "outer", bit, backward)
    low = inner_bits[0]
    counted = partner_counts("inner", low, backward)
    known = added(rows_before + earlier_b, group_b)
    sent = jnp.where(counted, known, known + group_b)
    earlier_a = added(earlier_a, group_a)
    got_b = swap(sent, "inner", low)
    if backward:
        return known, got_b, earlier_a
    return jnp.concatenate([earlier_a, known + got_b], axis=0)


def tail_kernel(
    scaling, lower_known, lower_got, upper_later, local_k, local_v, value, key, out_k, out_v
):
    half = HEADS // 2
    for h in range(HEADS):
        later = lower_known[h] + lower_got[h] if h < half else upper_later[h - half]
        later_half = later.astype(jnp.bfloat16)
        cols = slice(h * HEAD, (h + 1) * HEAD)
        from_later_k = lax.dot_general(
            value[:, cols], later_half, (((1,), (1,)), ((), ())), preferred_element_type=jnp.float32
        )
        out_k[:, cols] = (scaling * (local_k[h] + from_later_k)).astype(out_k.dtype)
        from_later_v = lax.dot_general(
            key[:, cols], later_half, (((1,), (0,)), ((), ())), preferred_element_type=jnp.float32
        )
        out_v[:, cols] = (local_v[h] + scaling * from_later_v).astype(out_v.dtype)


def tail(lower_known, lower_got, upper_later, local_k, local_v, value, key):
    rows = value.shape[0]
    vmem = pl.BlockSpec(memory_space=pltpu.VMEM)
    out = jax.ShapeDtypeStruct((rows, HEADS * HEAD), jnp.bfloat16)
    return pl.pallas_call(
        functools.partial(tail_kernel, HEAD ** (-0.5)),
        out_shape=(out, out),
        in_specs=[vmem] * 7,
        out_specs=(vmem, vmem),
        cost_estimate=pl.CostEstimate(
            flops=4 * HEADS * rows * HEAD * HEAD, transcendentals=0, bytes_accessed=12 * rows * 1024 * 4
        ),
    )(lower_known, lower_got, upper_later, local_k, local_v, value, key)


def state_kernel(key, value, out):
    for h in range(HEADS):
        cols = slice(h * HEAD, (h + 1) * HEAD)
        out[h] = lax.dot_general(
            key[:, cols], value[:, cols], (((0,), (0,)), ((), ())), preferred_element_type=jnp.float32
        )


def key_value_state(key, value):
    vmem = pl.BlockSpec(memory_space=pltpu.VMEM)
    return pl.pallas_call(
        state_kernel,
        out_shape=jax.ShapeDtypeStruct((HEADS, HEAD, HEAD), jnp.float32),
        in_specs=[vmem, vmem],
        out_specs=vmem,
        cost_estimate=pl.CostEstimate(
            flops=2 * HEADS * key.shape[0] * HEAD * HEAD, transcendentals=0, bytes_accessed=4 * key.size * 2
        ),
    )(key, value)


def per_device(query, key, value, grad_out):
    rows_dev = query.shape[0]
    scaling = HEAD ** (-0.5)
    queries = query.reshape(rows_dev, HEADS, HEAD)
    key_rows = key.reshape(rows_dev, HEADS, HEAD)
    value_rows = value.reshape(rows_dev, HEADS, HEAD)
    line = lax.broadcasted_iota(jnp.int32, (rows_dev, rows_dev), 0)
    column = lax.broadcasted_iota(jnp.int32, (rows_dev, rows_dev), 1)
    causal = (line >= column)[None]
    state = key_value_state(key, value)
    prior = chunked_scan(state, False)
    prior_half = prior.astype(jnp.bfloat16)
    scores = (
        jnp.einsum("thi,shi->hts", queries, key_rows, preferred_element_type=jnp.float32) * scaling
    )
    score_half = jnp.where(causal, scores, 0.0).astype(jnp.bfloat16)
    attended = jnp.einsum(
        "hts,shj->thj", score_half, value_rows, preferred_element_type=jnp.float32
    )
    attended = attended + scaling * jnp.einsum(
        "thi,hij->thj", queries, prior_half, preferred_element_type=jnp.float32
    )
    flat = attended.reshape(rows_dev, HEADS * HEAD)
    inverse = lax.rsqrt(jnp.mean(flat * flat, axis=-1, keepdims=True) + 1e-05)
    normed = flat * inverse
    grads_flat = grad_out.astype(jnp.float32)
    grad_pre = inverse * (
        grads_flat - normed * jnp.mean(grads_flat * normed, axis=-1, keepdims=True)
    )
    grad_half = grad_pre.astype(jnp.bfloat16).reshape(rows_dev, HEADS, HEAD)
    dscores = jnp.einsum("thj,shj->hts", grad_half, value_rows, preferred_element_type=jnp.float32)
    dscore_half = jnp.where(causal, dscores, 0.0).astype(jnp.bfloat16)
    grad_q = jnp.einsum("hts,shi->thi", dscore_half, key_rows, preferred_element_type=jnp.float32)
    grad_q = scaling * (
        grad_q
        + jnp.einsum("thj,hij->thi", grad_half, prior_half, preferred_element_type=jnp.float32)
    )
    grad_state = jnp.einsum("thi,thj->hij", queries, grad_half, preferred_element_type=jnp.float32)
    lower_known, lower_got, upper_later = chunked_scan(grad_state, True)
    local_k = jnp.einsum("hts,thi->hsi", dscore_half, queries, preferred_element_type=jnp.float32)
    local_v = jnp.einsum("hts,thj->hsj", score_half, grad_half, preferred_element_type=jnp.float32)
    grad_k, grad_v = tail(lower_known, lower_got, upper_later, local_k, local_v, value, key)
    width = HEADS * HEAD
    return (
        normed.astype(jnp.bfloat16),
        grad_q.reshape(rows_dev, width).astype(jnp.bfloat16),
        grad_k,
        grad_v,
    )


def solution(mesh):
    placed = P(("grp", "outer", "inner"), None)
    return jax.shard_map(
        per_device,
        mesh=mesh,
        in_specs=(placed, placed, placed, placed),
        out_specs=(placed, placed, placed, placed),
        check_vma=False,
    )
```

```python
import functools

import jax
import jax.numpy as jnp
from jax import lax
from jax.experimental import pallas as pl
from jax.experimental.pallas import tpu as pltpu
from jax.sharding import PartitionSpec as P

HEADS = 8
HEAD = 128


def axis_bits(axis):
    count = lax.axis_size(axis)
    return [1 << k for k in range(count.bit_length() - 1)]


def swap(value, axis, bit):
    count = lax.axis_size(axis)
    return lax.ppermute(value, axis, [(i, i ^ bit) for i in range(count)])


def partner_counts(axis, bit, backward):
    partner_lower = (lax.axis_index(axis) & bit) != 0
    return jnp.logical_not(partner_lower) if backward else partner_lower


def subcube_step(earlier, total, axis, bit, backward):
    got = swap(total, axis, bit)
    counted = partner_counts(axis, bit, backward)
    return earlier + [jnp.where(counted, got, 0.0)], total + got


def added(pieces, like):
    total = jnp.zeros_like(like)
    for piece in pieces:
        total = total + piece
    return total


def scan_inner_first(value, backward):
    earlier, total = [], value
    for axis in ("inner", "outer"):
        for bit in axis_bits(axis):
            earlier, total = subcube_step(earlier, total, axis, bit, backward)
    return added(earlier, value)


def chunked_scan(value, backward):
    half = value.shape[0] // 2
    group_a, group_b = value[:half], value[half:]
    inner_bits, outer_bits = axis_bits("inner"), axis_bits("outer")
    if not inner_bits:
        result = scan_inner_first(value, backward)
        if backward:
            return result[:half], result[half:], jnp.zeros_like(result[half:])
        return result
    earlier_a, total_a = subcube_step([], group_a, "inner", inner_bits[0], backward)
    earlier_b, total_b = [], group_b
    for bit in inner_bits[1:]:
        earlier_b, total_b = subcube_step(earlier_b, total_b, "inner", bit, backward)
    (earlier_b, total_b), _ = lax.optimization_barrier(((earlier_b, total_b), total_a))
    rows_before, rows_total = [], total_b
    for index, bit in enumerate(outer_bits):
        rows_before, rows_total = subcube_step(rows_before, rows_total, "outer", bit, backward)
        if index == 0 and not backward:
            (earlier_a, total_a), _ = lax.optimization_barrier(((earlier_a, total_a), rows_total))
    for bit in inner_bits[1:]:
        earlier_a, total_a = subcube_step(earlier_a, total_a, "inner", bit, backward)
    for bit in outer_bits:
        earlier_a, total_a = subcube_step(earlier_a, total_a, "outer", bit, backward)
    low = inner_bits[0]
    counted = partner_counts("inner", low, backward)
    known = added(rows_before + earlier_b, group_b)
    sent = jnp.where(counted, known, known + group_b)
    earlier_a = added(earlier_a, group_a)
    got_b = swap(sent, "inner", low)
    if backward:
        return earlier_a, known, got_b
    return jnp.concatenate([earlier_a, known + got_b], axis=0)


def tail_kernel(
    scaling, lower_later, upper_known, upper_got, local_k, local_v, value, key, out_k, out_v
):
    half = HEADS // 2
    for h in range(HEADS):
        later = lower_later[h] if h < half else upper_known[h - half] + upper_got[h - half]
        later_half = later.astype(jnp.bfloat16)
        cols = slice(h * HEAD, (h + 1) * HEAD)
        from_later_k = lax.dot_general(
            value[:, cols], later_half, (((1,), (1,)), ((), ())), preferred_element_type=jnp.float32
        )
        out_k[:, cols] = (scaling * (local_k[h] + from_later_k)).astype(out_k.dtype)
        from_later_v = lax.dot_general(
            key[:, cols], later_half, (((1,), (0,)), ((), ())), preferred_element_type=jnp.float32
        )
        out_v[:, cols] = (local_v[h] + scaling * from_later_v).astype(out_v.dtype)


def tail(lower_later, upper_known, upper_got, local_k, local_v, value, key):
    rows = value.shape[0]
    vmem = pl.BlockSpec(memory_space=pltpu.VMEM)
    out = jax.ShapeDtypeStruct((rows, HEADS * HEAD), jnp.bfloat16)
    return pl.pallas_call(
        functools.partial(tail_kernel, HEAD ** (-0.5)),
        out_shape=(out, out),
        in_specs=[vmem] * 7,
        out_specs=(vmem, vmem),
        cost_estimate=pl.CostEstimate(
            flops=4 * HEADS * rows * HEAD * HEAD, transcendentals=0, bytes_accessed=12 * rows * 1024 * 4
        ),
    )(lower_later, upper_known, upper_got, local_k, local_v, value, key)


def per_device(query, key, value, grad_out):
    rows_dev = query.shape[0]
    scaling = HEAD ** (-0.5)
    queries = query.reshape(rows_dev, HEADS, HEAD)
    key_rows = key.reshape(rows_dev, HEADS, HEAD)
    value_rows = value.reshape(rows_dev, HEADS, HEAD)
    line = lax.broadcasted_iota(jnp.int32, (rows_dev, rows_dev), 0)
    column = lax.broadcasted_iota(jnp.int32, (rows_dev, rows_dev), 1)
    causal = (line >= column)[None]
    state = jnp.einsum("thi,thj->hij", key_rows, value_rows, preferred_element_type=jnp.float32)
    prior = chunked_scan(state, False)
    prior_half = prior.astype(jnp.bfloat16)
    scores = (
        jnp.einsum("thi,shi->hts", queries, key_rows, preferred_element_type=jnp.float32) * scaling
    )
    score_half = jnp.where(causal, scores, 0.0).astype(jnp.bfloat16)
    attended = jnp.einsum(
        "hts,shj->thj", score_half, value_rows, preferred_element_type=jnp.float32
    )
    attended = attended + scaling * jnp.einsum(
        "thi,hij->thj", queries, prior_half, preferred_element_type=jnp.float32
    )
    flat = attended.reshape(rows_dev, HEADS * HEAD)
    inverse = lax.rsqrt(jnp.mean(flat * flat, axis=-1, keepdims=True) + 1e-05)
    normed = flat * inverse
    grads_flat = grad_out.astype(jnp.float32)
    grad_pre = inverse * (
        grads_flat - normed * jnp.mean(grads_flat * normed, axis=-1, keepdims=True)
    )
    grad_half = grad_pre.astype(jnp.bfloat16).reshape(rows_dev, HEADS, HEAD)
    dscores = jnp.einsum("thj,shj->hts", grad_half, value_rows, preferred_element_type=jnp.float32)
    dscore_half = jnp.where(causal, dscores, 0.0).astype(jnp.bfloat16)
    grad_q = jnp.einsum("hts,shi->thi", dscore_half, key_rows, preferred_element_type=jnp.float32)
    grad_q = scaling * (
        grad_q
        + jnp.einsum("thj,hij->thi", grad_half, prior_half, preferred_element_type=jnp.float32)
    )
    grad_state = jnp.einsum("thi,thj->hij", queries, grad_half, preferred_element_type=jnp.float32)
    lower_later, upper_known, upper_got = chunked_scan(grad_state, True)
    local_k = jnp.einsum("hts,thi->hsi", dscore_half, queries, preferred_element_type=jnp.float32)
    local_v = jnp.einsum("hts,thj->hsj", score_half, grad_half, preferred_element_type=jnp.float32)
    grad_k, grad_v = tail(lower_later, upper_known, upper_got, local_k, local_v, value, key)
    width = HEADS * HEAD
    return (
        normed.astype(jnp.bfloat16),
        grad_q.reshape(rows_dev, width).astype(jnp.bfloat16),
        grad_k,
        grad_v,
    )


def solution(mesh):
    placed = P(("grp", "outer", "inner"), None)
    return jax.shard_map(
        per_device,
        mesh=mesh,
        in_specs=(placed, placed, placed, placed),
        out_specs=(placed, placed, placed, placed),
        check_vma=False,
    )
```

```python
import functools

import jax
import jax.numpy as jnp
from jax import lax
from jax.experimental import pallas as pl
from jax.experimental.pallas import tpu as pltpu
from jax.sharding import PartitionSpec as P

HEADS = 8
HEAD = 128


def axis_bits(axis):
    count = lax.axis_size(axis)
    return [1 << k for k in range(count.bit_length() - 1)]


def swap(value, axis, bit):
    count = lax.axis_size(axis)
    return lax.ppermute(value, axis, [(i, i ^ bit) for i in range(count)])


def partner_counts(axis, bit, backward):
    partner_lower = (lax.axis_index(axis) & bit) != 0
    return jnp.logical_not(partner_lower) if backward else partner_lower


def subcube_step(earlier, total, axis, bit, backward):
    got = swap(total, axis, bit)
    counted = partner_counts(axis, bit, backward)
    return earlier + [jnp.where(counted, got, 0.0)], total + got


def added(pieces, like):
    total = jnp.zeros_like(like)
    for piece in pieces:
        total = total + piece
    return total


def scan_inner_first(value, backward):
    earlier, total = [], value
    for axis in ("inner", "outer"):
        for bit in axis_bits(axis):
            earlier, total = subcube_step(earlier, total, axis, bit, backward)
    return added(earlier, value)


def chunked_scan(value, backward, passenger=None):
    half = value.shape[0] // 2
    group_a, group_b = value[:half], value[half:]
    if backward:
        group_a, group_b = group_b, group_a
    inner_bits, outer_bits = axis_bits("inner"), axis_bits("outer")
    if not inner_bits:
        result = scan_inner_first(value, backward)
        if backward:
            return result[:half], jnp.zeros_like(result[:half]), result[half:]
        return result, passenger
    earlier_a, total_a = subcube_step([], group_a, "inner", inner_bits[0], backward)
    earlier_b, total_b = [], group_b
    for bit in inner_bits[1:]:
        earlier_b, total_b = subcube_step(earlier_b, total_b, "inner", bit, backward)
    (earlier_b, total_b), _ = lax.optimization_barrier(((earlier_b, total_b), total_a))
    rows_before, rows_total = [], total_b
    for index, bit in enumerate(outer_bits):
        rows_before, rows_total = subcube_step(rows_before, rows_total, "outer", bit, backward)
        if index == 0 and not backward:
            (earlier_a, total_a), _, passenger = lax.optimization_barrier(
                ((earlier_a, total_a), rows_total, passenger)
            )
    for bit in inner_bits[1:]:
        earlier_a, total_a = subcube_step(earlier_a, total_a, "inner", bit, backward)
    for bit in outer_bits:
        earlier_a, total_a = subcube_step(earlier_a, total_a, "outer", bit, backward)
    low = inner_bits[0]
    counted = partner_counts("inner", low, backward)
    known = added(rows_before + earlier_b, group_b)
    sent = jnp.where(counted, known, known + group_b)
    earlier_a = added(earlier_a, group_a)
    got_b = swap(sent, "inner", low)
    if backward:
        return known, got_b, earlier_a
    return jnp.concatenate([earlier_a, known + got_b], axis=0), passenger


def tail_kernel(
    scaling, lower_known, lower_got, upper_later, local_k, local_v, value, key, out_k, out_v
):
    half = HEADS // 2
    for h in range(HEADS):
        later = lower_known[h] + lower_got[h] if h < half else upper_later[h - half]
        later_half = later.astype(jnp.bfloat16)
        cols = slice(h * HEAD, (h + 1) * HEAD)
        from_later_k = lax.dot_general(
            value[:, cols], later_half, (((1,), (1,)), ((), ())), preferred_element_type=jnp.float32
        )
        out_k[:, cols] = (scaling * (local_k[h] + from_later_k)).astype(out_k.dtype)
        from_later_v = lax.dot_general(
            key[:, cols], later_half, (((1,), (0,)), ((), ())), preferred_element_type=jnp.float32
        )
        out_v[:, cols] = (local_v[h] + scaling * from_later_v).astype(out_v.dtype)


def tail(lower_known, lower_got, upper_later, local_k, local_v, value, key):
    rows = value.shape[0]
    vmem = pl.BlockSpec(memory_space=pltpu.VMEM)
    out = jax.ShapeDtypeStruct((rows, HEADS * HEAD), jnp.bfloat16)
    return pl.pallas_call(
        functools.partial(tail_kernel, HEAD ** (-0.5)),
        out_shape=(out, out),
        in_specs=[vmem] * 7,
        out_specs=(vmem, vmem),
        cost_estimate=pl.CostEstimate(
            flops=4 * HEADS * rows * HEAD * HEAD, transcendentals=0, bytes_accessed=12 * rows * 1024 * 4
        ),
    )(lower_known, lower_got, upper_later, local_k, local_v, value, key)


def per_device(query, key, value, grad_out):
    rows_dev = query.shape[0]
    scaling = HEAD ** (-0.5)
    queries = query.reshape(rows_dev, HEADS, HEAD)
    key_rows = key.reshape(rows_dev, HEADS, HEAD)
    value_rows = value.reshape(rows_dev, HEADS, HEAD)
    line = lax.broadcasted_iota(jnp.int32, (rows_dev, rows_dev), 0)
    column = lax.broadcasted_iota(jnp.int32, (rows_dev, rows_dev), 1)
    causal = (line >= column)[None]
    state = jnp.einsum("thi,thj->hij", key_rows, value_rows, preferred_element_type=jnp.float32)
    prior, grads_flat = chunked_scan(state, False, grad_out.astype(jnp.float32))
    prior_half = prior.astype(jnp.bfloat16)
    scores = (
        jnp.einsum("thi,shi->hts", queries, key_rows, preferred_element_type=jnp.float32) * scaling
    )
    score_half = jnp.where(causal, scores, 0.0).astype(jnp.bfloat16)
    attended = jnp.einsum(
        "hts,shj->thj", score_half, value_rows, preferred_element_type=jnp.float32
    )
    attended = attended + scaling * jnp.einsum(
        "thi,hij->thj", queries, prior_half, preferred_element_type=jnp.float32
    )
    flat = attended.reshape(rows_dev, HEADS * HEAD)
    inverse = lax.rsqrt(jnp.mean(flat * flat, axis=-1, keepdims=True) + 1e-05)
    normed = flat * inverse
    grad_pre = inverse * (
        grads_flat - normed * jnp.mean(grads_flat * normed, axis=-1, keepdims=True)
    )
    grad_half = grad_pre.astype(jnp.bfloat16).reshape(rows_dev, HEADS, HEAD)
    dscores = jnp.einsum("thj,shj->hts", grad_half, value_rows, preferred_element_type=jnp.float32)
    dscore_half = jnp.where(causal, dscores, 0.0).astype(jnp.bfloat16)
    grad_q = jnp.einsum("hts,shi->thi", dscore_half, key_rows, preferred_element_type=jnp.float32)
    grad_q = scaling * (
        grad_q
        + jnp.einsum("thj,hij->thi", grad_half, prior_half, preferred_element_type=jnp.float32)
    )
    grad_state = jnp.einsum("thi,thj->hij", queries, grad_half, preferred_element_type=jnp.float32)
    lower_known, lower_got, upper_later = chunked_scan(grad_state, True)
    local_k = jnp.einsum("hts,thi->hsi", dscore_half, queries, preferred_element_type=jnp.float32)
    local_v = jnp.einsum("hts,thj->hsj", score_half, grad_half, preferred_element_type=jnp.float32)
    grad_k, grad_v = tail(lower_known, lower_got, upper_later, local_k, local_v, value, key)
    width = HEADS * HEAD
    return (
        normed.astype(jnp.bfloat16),
        grad_q.reshape(rows_dev, width).astype(jnp.bfloat16),
        grad_k,
        grad_v,
    )


def solution(mesh):
    placed = P(("grp", "outer", "inner"), None)
    return jax.shard_map(
        per_device,
        mesh=mesh,
        in_specs=(placed, placed, placed, placed),
        out_specs=(placed, placed, placed, placed),
        check_vma=False,
    )
```

```python
import functools

import jax
import jax.numpy as jnp
from jax import lax
from jax.experimental import pallas as pl
from jax.experimental.pallas import tpu as pltpu
from jax.sharding import PartitionSpec as P

HEADS = 8
HEAD = 128


def axis_bits(axis):
    count = lax.axis_size(axis)
    return [1 << k for k in range(count.bit_length() - 1)]


def swap(value, axis, bit):
    count = lax.axis_size(axis)
    return lax.ppermute(value, axis, [(i, i ^ bit) for i in range(count)])


def partner_counts(axis, bit, backward):
    partner_lower = (lax.axis_index(axis) & bit) != 0
    return jnp.logical_not(partner_lower) if backward else partner_lower


def subcube_step(earlier, total, axis, bit, backward):
    got = swap(total, axis, bit)
    counted = partner_counts(axis, bit, backward)
    return earlier + [jnp.where(counted, got, 0.0)], total + got


def added(pieces, like):
    total = jnp.zeros_like(like)
    for piece in pieces:
        total = total + piece
    return total


def scan_inner_first(value, backward):
    earlier, total = [], value
    for axis in ("inner", "outer"):
        for bit in axis_bits(axis):
            earlier, total = subcube_step(earlier, total, axis, bit, backward)
    return added(earlier, value)


def chunked_scan(value, backward, passenger=None):
    half = value.shape[0] // 2
    group_a, group_b = value[:half], value[half:]
    if backward:
        group_a, group_b = group_b, group_a
    inner_bits, outer_bits = axis_bits("inner"), axis_bits("outer")
    if not inner_bits:
        result = scan_inner_first(value, backward)
        if backward:
            return result[:half], jnp.zeros_like(result[:half]), result[half:], passenger
        return result
    earlier_a, total_a = subcube_step([], group_a, "inner", inner_bits[0], backward)
    earlier_b, total_b = [], group_b
    for bit in inner_bits[1:]:
        earlier_b, total_b = subcube_step(earlier_b, total_b, "inner", bit, backward)
    (earlier_b, total_b), _, passenger = lax.optimization_barrier(
        ((earlier_b, total_b), total_a, passenger)
    )
    rows_before, rows_total = [], total_b
    for index, bit in enumerate(outer_bits):
        rows_before, rows_total = subcube_step(rows_before, rows_total, "outer", bit, backward)
        if index == 0 and not backward:
            (earlier_a, total_a), _ = lax.optimization_barrier(((earlier_a, total_a), rows_total))
    for bit in inner_bits[1:]:
        earlier_a, total_a = subcube_step(earlier_a, total_a, "inner", bit, backward)
    for bit in outer_bits:
        earlier_a, total_a = subcube_step(earlier_a, total_a, "outer", bit, backward)
    low = inner_bits[0]
    counted = partner_counts("inner", low, backward)
    known = added(rows_before + earlier_b, group_b)
    sent = jnp.where(counted, known, known + group_b)
    earlier_a = added(earlier_a, group_a)
    got_b = swap(sent, "inner", low)
    if backward:
        return known, got_b, earlier_a, passenger
    return jnp.concatenate([earlier_a, known + got_b], axis=0)


def tail_kernel(
    scaling, lower_known, lower_got, upper_later, local_k, local_v, value, key, out_k, out_v
):
    half = HEADS // 2
    for h in range(HEADS):
        later = lower_known[h] + lower_got[h] if h < half else upper_later[h - half]
        later_half = later.astype(jnp.bfloat16)
        cols = slice(h * HEAD, (h + 1) * HEAD)
        from_later_k = lax.dot_general(
            value[:, cols], later_half, (((1,), (1,)), ((), ())), preferred_element_type=jnp.float32
        )
        out_k[:, cols] = (scaling * (local_k[h] + from_later_k)).astype(out_k.dtype)
        from_later_v = lax.dot_general(
            key[:, cols], later_half, (((1,), (0,)), ((), ())), preferred_element_type=jnp.float32
        )
        out_v[:, cols] = (local_v[h] + scaling * from_later_v).astype(out_v.dtype)


def tail(lower_known, lower_got, upper_later, local_k, local_v, value, key):
    rows = value.shape[0]
    vmem = pl.BlockSpec(memory_space=pltpu.VMEM)
    out = jax.ShapeDtypeStruct((rows, HEADS * HEAD), jnp.bfloat16)
    return pl.pallas_call(
        functools.partial(tail_kernel, HEAD ** (-0.5)),
        out_shape=(out, out),
        in_specs=[vmem] * 7,
        out_specs=(vmem, vmem),
        cost_estimate=pl.CostEstimate(
            flops=4 * HEADS * rows * HEAD * HEAD, transcendentals=0, bytes_accessed=12 * rows * 1024 * 4
        ),
    )(lower_known, lower_got, upper_later, local_k, local_v, value, key)


def per_device(query, key, value, grad_out):
    rows_dev = query.shape[0]
    scaling = HEAD ** (-0.5)
    queries = query.reshape(rows_dev, HEADS, HEAD)
    key_rows = key.reshape(rows_dev, HEADS, HEAD)
    value_rows = value.reshape(rows_dev, HEADS, HEAD)
    line = lax.broadcasted_iota(jnp.int32, (rows_dev, rows_dev), 0)
    column = lax.broadcasted_iota(jnp.int32, (rows_dev, rows_dev), 1)
    causal = (line >= column)[None]
    state = jnp.einsum("thi,thj->hij", key_rows, value_rows, preferred_element_type=jnp.float32)
    prior = chunked_scan(state, False)
    prior_half = prior.astype(jnp.bfloat16)
    scores = (
        jnp.einsum("thi,shi->hts", queries, key_rows, preferred_element_type=jnp.float32) * scaling
    )
    score_half = jnp.where(causal, scores, 0.0).astype(jnp.bfloat16)
    attended = jnp.einsum(
        "hts,shj->thj", score_half, value_rows, preferred_element_type=jnp.float32
    )
    attended = attended + scaling * jnp.einsum(
        "thi,hij->thj", queries, prior_half, preferred_element_type=jnp.float32
    )
    flat = attended.reshape(rows_dev, HEADS * HEAD)
    inverse = lax.rsqrt(jnp.mean(flat * flat, axis=-1, keepdims=True) + 1e-05)
    normed = flat * inverse
    grads_flat = grad_out.astype(jnp.float32)
    grad_pre = inverse * (
        grads_flat - normed * jnp.mean(grads_flat * normed, axis=-1, keepdims=True)
    )
    grad_half = grad_pre.astype(jnp.bfloat16).reshape(rows_dev, HEADS, HEAD)
    dscores = jnp.einsum("thj,shj->hts", grad_half, value_rows, preferred_element_type=jnp.float32)
    dscore_half = jnp.where(causal, dscores, 0.0).astype(jnp.bfloat16)
    grad_q = jnp.einsum("hts,shi->thi", dscore_half, key_rows, preferred_element_type=jnp.float32)
    grad_q = scaling * (
        grad_q
        + jnp.einsum("thj,hij->thi", grad_half, prior_half, preferred_element_type=jnp.float32)
    )
    grad_state = jnp.einsum("thi,thj->hij", queries, grad_half, preferred_element_type=jnp.float32)
    local_k = jnp.einsum("hts,thi->hsi", dscore_half, queries, preferred_element_type=jnp.float32)
    local_v = jnp.einsum("hts,thj->hsj", score_half, grad_half, preferred_element_type=jnp.float32)
    lower_known, lower_got, upper_later, local_k = chunked_scan(grad_state, True, local_k)
    grad_k, grad_v = tail(lower_known, lower_got, upper_later, local_k, local_v, value, key)
    width = HEADS * HEAD
    return (
        normed.astype(jnp.bfloat16),
        grad_q.reshape(rows_dev, width).astype(jnp.bfloat16),
        grad_k,
        grad_v,
    )


def solution(mesh):
    placed = P(("grp", "outer", "inner"), None)
    return jax.shard_map(
        per_device,
        mesh=mesh,
        in_specs=(placed, placed, placed, placed),
        out_specs=(placed, placed, placed, placed),
        check_vma=False,
    )
```

```python
import functools

import jax
import jax.numpy as jnp
from jax import lax
from jax.experimental import pallas as pl
from jax.experimental.pallas import tpu as pltpu
from jax.sharding import PartitionSpec as P

HEADS = 8
HEAD = 128


def axis_bits(axis):
    count = lax.axis_size(axis)
    return [1 << k for k in range(count.bit_length() - 1)]


def swap(value, axis, bit):
    count = lax.axis_size(axis)
    return lax.ppermute(value, axis, [(i, i ^ bit) for i in range(count)])


def partner_counts(axis, bit, backward):
    partner_lower = (lax.axis_index(axis) & bit) != 0
    return jnp.logical_not(partner_lower) if backward else partner_lower


def subcube_step(earlier, total, axis, bit, backward):
    got = swap(total, axis, bit)
    counted = partner_counts(axis, bit, backward)
    return earlier + [jnp.where(counted, got, 0.0)], total + got


def added(pieces, like):
    total = jnp.zeros_like(like)
    for piece in pieces:
        total = total + piece
    return total


def scan_inner_first(value, backward):
    earlier, total = [], value
    for axis in ("inner", "outer"):
        for bit in axis_bits(axis):
            earlier, total = subcube_step(earlier, total, axis, bit, backward)
    return added(earlier, value)


def chunked_scan(value, backward):
    half = value.shape[0] // 2
    group_a, group_b = value[:half], value[half:]
    if backward:
        group_a, group_b = group_b, group_a
    inner_bits, outer_bits = axis_bits("inner"), axis_bits("outer")
    if not inner_bits:
        result = scan_inner_first(value, backward)
        if backward:
            return result[:half], jnp.zeros_like(result[:half]), result[half:]
        return result
    earlier_a, total_a = subcube_step([], group_a, "inner", inner_bits[0], backward)
    earlier_b, total_b = [], group_b
    for bit in inner_bits[1:]:
        earlier_b, total_b = subcube_step(earlier_b, total_b, "inner", bit, backward)
    (earlier_b, total_b), _ = lax.optimization_barrier(((earlier_b, total_b), total_a))
    rows_before, rows_total = [], total_b
    for index, bit in enumerate(outer_bits):
        rows_before, rows_total = subcube_step(rows_before, rows_total, "outer", bit, backward)
        if index == 0 and not backward:
            (earlier_a, total_a), _ = lax.optimization_barrier(((earlier_a, total_a), rows_total))
    for bit in inner_bits[1:]:
        earlier_a, total_a = subcube_step(earlier_a, total_a, "inner", bit, backward)
    for bit in outer_bits:
        earlier_a, total_a = subcube_step(earlier_a, total_a, "outer", bit, backward)
    low = inner_bits[0]
    counted = partner_counts("inner", low, backward)
    known = added(rows_before + earlier_b, group_b)
    sent = jnp.where(counted, known, known + group_b)
    earlier_a = added(earlier_a, group_a)
    got_b = swap(sent, "inner", low)
    if backward:
        return known, got_b, earlier_a
    return jnp.concatenate([earlier_a, known + got_b], axis=0)


def tail_kernel(
    scaling, lower_known, lower_got, upper_later, dscore, score, query, grad, value, key, out_k, out_v
):
    half = HEADS // 2
    for h in range(HEADS):
        later = lower_known[h] + lower_got[h] if h < half else upper_later[h - half]
        later_half = later.astype(jnp.bfloat16)
        cols = slice(h * HEAD, (h + 1) * HEAD)
        from_later_k = lax.dot_general(
            value[:, cols], later_half, (((1,), (1,)), ((), ())), preferred_element_type=jnp.float32
        )
        local_k = lax.dot_general(
            dscore[h], query[:, cols], (((0,), (0,)), ((), ())), preferred_element_type=jnp.float32
        )
        out_k[:, cols] = (scaling * (local_k + from_later_k)).astype(out_k.dtype)
        from_later_v = lax.dot_general(
            key[:, cols], later_half, (((1,), (0,)), ((), ())), preferred_element_type=jnp.float32
        )
        local_v = lax.dot_general(
            score[h], grad[:, cols], (((0,), (0,)), ((), ())), preferred_element_type=jnp.float32
        )
        out_v[:, cols] = (local_v + scaling * from_later_v).astype(out_v.dtype)


def tail(lower_known, lower_got, upper_later, dscore, score, query, grad, value, key):
    rows = value.shape[0]
    vmem = pl.BlockSpec(memory_space=pltpu.VMEM)
    out = jax.ShapeDtypeStruct((rows, HEADS * HEAD), jnp.bfloat16)
    return pl.pallas_call(
        functools.partial(tail_kernel, HEAD ** (-0.5)),
        out_shape=(out, out),
        in_specs=[vmem] * 9,
        out_specs=(vmem, vmem),
        cost_estimate=pl.CostEstimate(
            flops=8 * HEADS * rows * HEAD * HEAD, transcendentals=0, bytes_accessed=12 * rows * 1024 * 4
        ),
    )(lower_known, lower_got, upper_later, dscore, score, query, grad, value, key)


def per_device(query, key, value, grad_out):
    rows_dev = query.shape[0]
    scaling = HEAD ** (-0.5)
    queries = query.reshape(rows_dev, HEADS, HEAD)
    key_rows = key.reshape(rows_dev, HEADS, HEAD)
    value_rows = value.reshape(rows_dev, HEADS, HEAD)
    line = lax.broadcasted_iota(jnp.int32, (rows_dev, rows_dev), 0)
    column = lax.broadcasted_iota(jnp.int32, (rows_dev, rows_dev), 1)
    causal = (line >= column)[None]
    state = jnp.einsum("thi,thj->hij", key_rows, value_rows, preferred_element_type=jnp.float32)
    prior = chunked_scan(state, False)
    prior_half = prior.astype(jnp.bfloat16)
    scores = (
        jnp.einsum("thi,shi->hts", queries, key_rows, preferred_element_type=jnp.float32) * scaling
    )
    score_half = jnp.where(causal, scores, 0.0).astype(jnp.bfloat16)
    attended = jnp.einsum(
        "hts,shj->thj", score_half, value_rows, preferred_element_type=jnp.float32
    )
    attended = attended + scaling * jnp.einsum(
        "thi,hij->thj", queries, prior_half, preferred_element_type=jnp.float32
    )
    flat = attended.reshape(rows_dev, HEADS * HEAD)
    inverse = lax.rsqrt(jnp.mean(flat * flat, axis=-1, keepdims=True) + 1e-05)
    normed = flat * inverse
    grads_flat = grad_out.astype(jnp.float32)
    grad_pre = inverse * (
        grads_flat - normed * jnp.mean(grads_flat * normed, axis=-1, keepdims=True)
    )
    grad_half = grad_pre.astype(jnp.bfloat16).reshape(rows_dev, HEADS, HEAD)
    dscores = jnp.einsum("thj,shj->hts", grad_half, value_rows, preferred_element_type=jnp.float32)
    dscore_half = jnp.where(causal, dscores, 0.0).astype(jnp.bfloat16)
    grad_q = jnp.einsum("hts,shi->thi", dscore_half, key_rows, preferred_element_type=jnp.float32)
    grad_q = scaling * (
        grad_q
        + jnp.einsum("thj,hij->thi", grad_half, prior_half, preferred_element_type=jnp.float32)
    )
    grad_state = jnp.einsum("thi,thj->hij", queries, grad_half, preferred_element_type=jnp.float32)
    lower_known, lower_got, upper_later = chunked_scan(grad_state, True)
    grad_k, grad_v = tail(
        lower_known,
        lower_got,
        upper_later,
        dscore_half,
        score_half,
        query,
        grad_half.reshape(rows_dev, HEADS * HEAD),
        value,
        key,
    )
    width = HEADS * HEAD
    return (
        normed.astype(jnp.bfloat16),
        grad_q.reshape(rows_dev, width).astype(jnp.bfloat16),
        grad_k,
        grad_v,
    )


def solution(mesh):
    placed = P(("grp", "outer", "inner"), None)
    return jax.shard_map(
        per_device,
        mesh=mesh,
        in_specs=(placed, placed, placed, placed),
        out_specs=(placed, placed, placed, placed),
        check_vma=False,
    )
```

```python
import functools

import jax
import jax.numpy as jnp
from jax import lax
from jax.experimental import pallas as pl
from jax.experimental.pallas import tpu as pltpu
from jax.sharding import PartitionSpec as P

HEADS = 8
HEAD = 128


def axis_bits(axis):
    count = lax.axis_size(axis)
    return [1 << k for k in range(count.bit_length() - 1)]


def swap(value, axis, bit):
    count = lax.axis_size(axis)
    return lax.ppermute(value, axis, [(i, i ^ bit) for i in range(count)])


def partner_counts(axis, bit, backward):
    partner_lower = (lax.axis_index(axis) & bit) != 0
    return jnp.logical_not(partner_lower) if backward else partner_lower


def subcube_step(earlier, total, axis, bit, backward):
    got = swap(total, axis, bit)
    counted = partner_counts(axis, bit, backward)
    return earlier + [jnp.where(counted, got, 0.0)], total + got


def added(pieces, like):
    total = jnp.zeros_like(like)
    for piece in pieces:
        total = total + piece
    return total


def scan_inner_first(value, backward):
    earlier, total = [], value
    for axis in ("inner", "outer"):
        for bit in axis_bits(axis):
            earlier, total = subcube_step(earlier, total, axis, bit, backward)
    return added(earlier, value)


def chunked_scan(value, backward):
    half = value.shape[0] // 2
    group_a, group_b = value[:half], value[half:]
    if backward:
        group_a, group_b = group_b, group_a
    inner_bits, outer_bits = axis_bits("inner"), axis_bits("outer")
    if not inner_bits:
        result = scan_inner_first(value, backward)
        if backward:
            return result[:half], jnp.zeros_like(result[:half]), result[half:]
        return result
    earlier_a, total_a = subcube_step([], group_a, "inner", inner_bits[0], backward)
    earlier_b, total_b = [], group_b
    for bit in inner_bits[1:]:
        earlier_b, total_b = subcube_step(earlier_b, total_b, "inner", bit, backward)
    (earlier_b, total_b), _ = lax.optimization_barrier(((earlier_b, total_b), total_a))
    rows_before, rows_total = [], total_b
    for index, bit in enumerate(outer_bits):
        rows_before, rows_total = subcube_step(rows_before, rows_total, "outer", bit, backward)
        if index == 0 and not backward:
            (earlier_a, total_a), _ = lax.optimization_barrier(((earlier_a, total_a), rows_total))
    for bit in inner_bits[1:]:
        earlier_a, total_a = subcube_step(earlier_a, total_a, "inner", bit, backward)
    for bit in outer_bits:
        earlier_a, total_a = subcube_step(earlier_a, total_a, "outer", bit, backward)
    low = inner_bits[0]
    counted = partner_counts("inner", low, backward)
    known = added(rows_before + earlier_b, group_b)
    sent = jnp.where(counted, known, known + group_b)
    earlier_a = added(earlier_a, group_a)
    got_b = swap(sent, "inner", low)
    if backward:
        return known, got_b, earlier_a
    return jnp.concatenate([earlier_a, known + got_b], axis=0)


def tail_kernel(scaling, lower_later, upper_later, local_k, local_v, value, key, out_k, out_v):
    half = HEADS // 2
    for h in range(HEADS):
        later = lower_later[h] if h < half else upper_later[h - half]
        later_half = later.astype(jnp.bfloat16)
        cols = slice(h * HEAD, (h + 1) * HEAD)
        from_later_k = lax.dot_general(
            value[:, cols], later_half, (((1,), (1,)), ((), ())), preferred_element_type=jnp.float32
        )
        out_k[:, cols] = (scaling * (local_k[h] + from_later_k)).astype(out_k.dtype)
        from_later_v = lax.dot_general(
            key[:, cols], later_half, (((1,), (0,)), ((), ())), preferred_element_type=jnp.float32
        )
        out_v[:, cols] = (local_v[h] + scaling * from_later_v).astype(out_v.dtype)


def tail(lower_later, upper_later, local_k, local_v, value, key):
    rows = value.shape[0]
    vmem = pl.BlockSpec(memory_space=pltpu.VMEM)
    out = jax.ShapeDtypeStruct((rows, HEADS * HEAD), jnp.bfloat16)
    return pl.pallas_call(
        functools.partial(tail_kernel, HEAD ** (-0.5)),
        out_shape=(out, out),
        in_specs=[vmem] * 6,
        out_specs=(vmem, vmem),
        cost_estimate=pl.CostEstimate(
            flops=4 * HEADS * rows * HEAD * HEAD, transcendentals=0, bytes_accessed=12 * rows * 1024 * 4
        ),
    )(lower_later, upper_later, local_k, local_v, value, key)


def per_device(query, key, value, grad_out):
    rows_dev = query.shape[0]
    scaling = HEAD ** (-0.5)
    queries = query.reshape(rows_dev, HEADS, HEAD)
    key_rows = key.reshape(rows_dev, HEADS, HEAD)
    value_rows = value.reshape(rows_dev, HEADS, HEAD)
    line = lax.broadcasted_iota(jnp.int32, (rows_dev, rows_dev), 0)
    column = lax.broadcasted_iota(jnp.int32, (rows_dev, rows_dev), 1)
    causal = (line >= column)[None]
    state = jnp.einsum("thi,thj->hij", key_rows, value_rows, preferred_element_type=jnp.float32)
    prior = chunked_scan(state, False)
    prior_half = prior.astype(jnp.bfloat16)
    scores = (
        jnp.einsum("thi,shi->hts", queries, key_rows, preferred_element_type=jnp.float32) * scaling
    )
    score_half = jnp.where(causal, scores, 0.0).astype(jnp.bfloat16)
    attended = jnp.einsum(
        "hts,shj->thj", score_half, value_rows, preferred_element_type=jnp.float32
    )
    attended = attended + scaling * jnp.einsum(
        "thi,hij->thj", queries, prior_half, preferred_element_type=jnp.float32
    )
    flat = attended.reshape(rows_dev, HEADS * HEAD)
    inverse = lax.rsqrt(jnp.mean(flat * flat, axis=-1, keepdims=True) + 1e-05)
    normed = flat * inverse
    grads_flat = grad_out.astype(jnp.float32)
    grad_pre = inverse * (
        grads_flat - normed * jnp.mean(grads_flat * normed, axis=-1, keepdims=True)
    )
    grad_half = grad_pre.astype(jnp.bfloat16).reshape(rows_dev, HEADS, HEAD)
    dscores = jnp.einsum("thj,shj->hts", grad_half, value_rows, preferred_element_type=jnp.float32)
    dscore_half = jnp.where(causal, dscores, 0.0).astype(jnp.bfloat16)
    grad_q = jnp.einsum("hts,shi->thi", dscore_half, key_rows, preferred_element_type=jnp.float32)
    grad_q = scaling * (
        grad_q
        + jnp.einsum("thj,hij->thi", grad_half, prior_half, preferred_element_type=jnp.float32)
    )
    grad_state = jnp.einsum("thi,thj->hij", queries, grad_half, preferred_element_type=jnp.float32)
    lower_known, lower_got, upper_later = chunked_scan(grad_state, True)
    local_k = jnp.einsum("hts,thi->hsi", dscore_half, queries, preferred_element_type=jnp.float32)
    local_v = jnp.einsum("hts,thj->hsj", score_half, grad_half, preferred_element_type=jnp.float32)
    grad_k, grad_v = tail(lower_known + lower_got, upper_later, local_k, local_v, value, key)
    width = HEADS * HEAD
    return (
        normed.astype(jnp.bfloat16),
        grad_q.reshape(rows_dev, width).astype(jnp.bfloat16),
        grad_k,
        grad_v,
    )


def solution(mesh):
    placed = P(("grp", "outer", "inner"), None)
    return jax.shard_map(
        per_device,
        mesh=mesh,
        in_specs=(placed, placed, placed, placed),
        out_specs=(placed, placed, placed, placed),
        check_vma=False,
    )
```

```python
import functools

import jax
import jax.numpy as jnp
from jax import lax
from jax.experimental import pallas as pl
from jax.experimental.pallas import tpu as pltpu
from jax.sharding import PartitionSpec as P

HEADS = 8
HEAD = 128


def axis_bits(axis):
    count = lax.axis_size(axis)
    return [1 << k for k in range(count.bit_length() - 1)]


def swap(value, axis, bit):
    count = lax.axis_size(axis)
    return lax.ppermute(value, axis, [(i, i ^ bit) for i in range(count)])


def partner_counts(axis, bit, backward):
    partner_lower = (lax.axis_index(axis) & bit) != 0
    return jnp.logical_not(partner_lower) if backward else partner_lower


def subcube_step(earlier, total, axis, bit, backward):
    got = swap(total, axis, bit)
    counted = partner_counts(axis, bit, backward)
    return earlier + [jnp.where(counted, got, 0.0)], total + got


def added(pieces, like):
    total = jnp.zeros_like(like)
    for piece in pieces:
        total = total + piece
    return total


def scan_inner_first(value, backward):
    earlier, total = [], value
    for axis in ("inner", "outer"):
        for bit in axis_bits(axis):
            earlier, total = subcube_step(earlier, total, axis, bit, backward)
    return added(earlier, value)


def chunked_scan(value, backward):
    half = value.shape[0] // 2
    group_a, group_b = value[:half], value[half:]
    if backward:
        group_a, group_b = group_b, group_a
    inner_bits, outer_bits = axis_bits("inner"), axis_bits("outer")
    if not inner_bits:
        result = scan_inner_first(value, backward)
        if backward:
            return result[:half], jnp.zeros_like(result[:half]), result[half:]
        return result
    earlier_a, total_a = subcube_step([], group_a, "inner", inner_bits[0], backward)
    earlier_b, total_b = [], group_b
    for bit in inner_bits[1:]:
        earlier_b, total_b = subcube_step(earlier_b, total_b, "inner", bit, backward)
    (earlier_b, total_b), _ = lax.optimization_barrier(((earlier_b, total_b), total_a))
    rows_before, rows_total = [], total_b
    if not backward:
        (earlier_a, total_a), _ = lax.optimization_barrier(((earlier_a, total_a), rows_total))
    for bit in outer_bits:
        rows_before, rows_total = subcube_step(rows_before, rows_total, "outer", bit, backward)
    for bit in inner_bits[1:]:
        earlier_a, total_a = subcube_step(earlier_a, total_a, "inner", bit, backward)
    for bit in outer_bits:
        earlier_a, total_a = subcube_step(earlier_a, total_a, "outer", bit, backward)
    low = inner_bits[0]
    counted = partner_counts("inner", low, backward)
    known = added(rows_before + earlier_b, group_b)
    sent = jnp.where(counted, known, known + group_b)
    earlier_a = added(earlier_a, group_a)
    got_b = swap(sent, "inner", low)
    if backward:
        return known, got_b, earlier_a
    return jnp.concatenate([earlier_a, known + got_b], axis=0)


def tail_kernel(scaling, lower_later, upper_later, local_k, local_v, value, key, out_k, out_v):
    half = HEADS // 2
    for h in range(HEADS):
        later = lower_later[h] if h < half else upper_later[h - half]
        later_half = later.astype(jnp.bfloat16)
        cols = slice(h * HEAD, (h + 1) * HEAD)
        from_later_k = lax.dot_general(
            value[:, cols], later_half, (((1,), (1,)), ((), ())), preferred_element_type=jnp.float32
        )
        out_k[:, cols] = (scaling * (local_k[h] + from_later_k)).astype(out_k.dtype)
        from_later_v = lax.dot_general(
            key[:, cols], later_half, (((1,), (0,)), ((), ())), preferred_element_type=jnp.float32
        )
        out_v[:, cols] = (local_v[h] + scaling * from_later_v).astype(out_v.dtype)


def tail(lower_later, upper_later, local_k, local_v, value, key):
    rows = value.shape[0]
    vmem = pl.BlockSpec(memory_space=pltpu.VMEM)
    out = jax.ShapeDtypeStruct((rows, HEADS * HEAD), jnp.bfloat16)
    return pl.pallas_call(
        functools.partial(tail_kernel, HEAD ** (-0.5)),
        out_shape=(out, out),
        in_specs=[vmem] * 6,
        out_specs=(vmem, vmem),
        cost_estimate=pl.CostEstimate(
            flops=4 * HEADS * rows * HEAD * HEAD, transcendentals=0, bytes_accessed=12 * rows * 1024 * 4
        ),
    )(lower_later, upper_later, local_k, local_v, value, key)


def per_device(query, key, value, grad_out):
    rows_dev = query.shape[0]
    scaling = HEAD ** (-0.5)
    queries = query.reshape(rows_dev, HEADS, HEAD)
    key_rows = key.reshape(rows_dev, HEADS, HEAD)
    value_rows = value.reshape(rows_dev, HEADS, HEAD)
    line = lax.broadcasted_iota(jnp.int32, (rows_dev, rows_dev), 0)
    column = lax.broadcasted_iota(jnp.int32, (rows_dev, rows_dev), 1)
    causal = (line >= column)[None]
    state = jnp.einsum("thi,thj->hij", key_rows, value_rows, preferred_element_type=jnp.float32)
    prior = chunked_scan(state, False)
    prior_half = prior.astype(jnp.bfloat16)
    scores = (
        jnp.einsum("thi,shi->hts", queries, key_rows, preferred_element_type=jnp.float32) * scaling
    )
    score_half = jnp.where(causal, scores, 0.0).astype(jnp.bfloat16)
    attended = jnp.einsum(
        "hts,shj->thj", score_half, value_rows, preferred_element_type=jnp.float32
    )
    attended = attended + scaling * jnp.einsum(
        "thi,hij->thj", queries, prior_half, preferred_element_type=jnp.float32
    )
    flat = attended.reshape(rows_dev, HEADS * HEAD)
    inverse = lax.rsqrt(jnp.mean(flat * flat, axis=-1, keepdims=True) + 1e-05)
    normed = flat * inverse
    grads_flat = grad_out.astype(jnp.float32)
    grad_pre = inverse * (
        grads_flat - normed * jnp.mean(grads_flat * normed, axis=-1, keepdims=True)
    )
    grad_half = grad_pre.astype(jnp.bfloat16).reshape(rows_dev, HEADS, HEAD)
    dscores = jnp.einsum("thj,shj->hts", grad_half, value_rows, preferred_element_type=jnp.float32)
    dscore_half = jnp.where(causal, dscores, 0.0).astype(jnp.bfloat16)
    grad_q = jnp.einsum("hts,shi->thi", dscore_half, key_rows, preferred_element_type=jnp.float32)
    grad_q = scaling * (
        grad_q
        + jnp.einsum("thj,hij->thi", grad_half, prior_half, preferred_element_type=jnp.float32)
    )
    grad_state = jnp.einsum("thi,thj->hij", queries, grad_half, preferred_element_type=jnp.float32)
    lower_known, lower_got, upper_later = chunked_scan(grad_state, True)
    local_k = jnp.einsum("hts,thi->hsi", dscore_half, queries, preferred_element_type=jnp.float32)
    local_v = jnp.einsum("hts,thj->hsj", score_half, grad_half, preferred_element_type=jnp.float32)
    grad_k, grad_v = tail(lower_known + lower_got, upper_later, local_k, local_v, value, key)
    width = HEADS * HEAD
    return (
        normed.astype(jnp.bfloat16),
        grad_q.reshape(rows_dev, width).astype(jnp.bfloat16),
        grad_k,
        grad_v,
    )


def solution(mesh):
    placed = P(("grp", "outer", "inner"), None)
    return jax.shard_map(
        per_device,
        mesh=mesh,
        in_specs=(placed, placed, placed, placed),
        out_specs=(placed, placed, placed, placed),
        check_vma=False,
    )
```

```python
import functools

import jax
import jax.numpy as jnp
from jax import lax
from jax.experimental import pallas as pl
from jax.experimental.pallas import tpu as pltpu
from jax.sharding import PartitionSpec as P

HEADS = 8
HEAD = 128


def axis_bits(axis):
    count = lax.axis_size(axis)
    return [1 << k for k in range(count.bit_length() - 1)]


def swap(value, axis, bit):
    count = lax.axis_size(axis)
    return lax.ppermute(value, axis, [(i, i ^ bit) for i in range(count)])


def partner_counts(axis, bit, backward):
    partner_lower = (lax.axis_index(axis) & bit) != 0
    return jnp.logical_not(partner_lower) if backward else partner_lower


def subcube_step(earlier, total, axis, bit, backward):
    got = swap(total, axis, bit)
    counted = partner_counts(axis, bit, backward)
    return earlier + [jnp.where(counted, got, 0.0)], total + got


def added(pieces, like):
    total = jnp.zeros_like(like)
    for piece in pieces:
        total = total + piece
    return total


def scan_inner_first(value, backward):
    earlier, total = [], value
    for axis in ("inner", "outer"):
        for bit in axis_bits(axis):
            earlier, total = subcube_step(earlier, total, axis, bit, backward)
    return added(earlier, value)


def chunked_scan(value, backward):
    half = value.shape[0] // 2
    group_a, group_b = value[:half], value[half:]
    if backward:
        group_a, group_b = group_b, group_a
    inner_bits, outer_bits = axis_bits("inner"), axis_bits("outer")
    if not inner_bits:
        result = scan_inner_first(value, backward)
        if backward:
            return result[:half], jnp.zeros_like(result[:half]), result[half:]
        return result
    earlier_a, total_a = subcube_step([], group_a, "inner", inner_bits[0], backward)
    earlier_b, total_b = [], group_b
    for bit in inner_bits[1:]:
        earlier_b, total_b = subcube_step(earlier_b, total_b, "inner", bit, backward)
    if not backward:
        (earlier_b, total_b), _ = lax.optimization_barrier(((earlier_b, total_b), total_a))
    rows_before, rows_total = [], total_b
    if not backward:
        (earlier_a, total_a), _ = lax.optimization_barrier(((earlier_a, total_a), rows_total))
    for bit in outer_bits:
        rows_before, rows_total = subcube_step(rows_before, rows_total, "outer", bit, backward)
    for bit in inner_bits[1:]:
        earlier_a, total_a = subcube_step(earlier_a, total_a, "inner", bit, backward)
    for bit in outer_bits:
        earlier_a, total_a = subcube_step(earlier_a, total_a, "outer", bit, backward)
    low = inner_bits[0]
    counted = partner_counts("inner", low, backward)
    known = added(rows_before + earlier_b, group_b)
    sent = jnp.where(counted, known, known + group_b)
    earlier_a = added(earlier_a, group_a)
    got_b = swap(sent, "inner", low)
    if backward:
        return known, got_b, earlier_a
    return jnp.concatenate([earlier_a, known + got_b], axis=0)


def tail_kernel(scaling, lower_later, upper_later, local_k, local_v, value, key, out_k, out_v):
    half = HEADS // 2
    for h in range(HEADS):
        later = lower_later[h] if h < half else upper_later[h - half]
        later_half = later.astype(jnp.bfloat16)
        cols = slice(h * HEAD, (h + 1) * HEAD)
        from_later_k = lax.dot_general(
            value[:, cols], later_half, (((1,), (1,)), ((), ())), preferred_element_type=jnp.float32
        )
        out_k[:, cols] = (scaling * (local_k[h] + from_later_k)).astype(out_k.dtype)
        from_later_v = lax.dot_general(
            key[:, cols], later_half, (((1,), (0,)), ((), ())), preferred_element_type=jnp.float32
        )
        out_v[:, cols] = (local_v[h] + scaling * from_later_v).astype(out_v.dtype)


def tail(lower_later, upper_later, local_k, local_v, value, key):
    rows = value.shape[0]
    vmem = pl.BlockSpec(memory_space=pltpu.VMEM)
    out = jax.ShapeDtypeStruct((rows, HEADS * HEAD), jnp.bfloat16)
    return pl.pallas_call(
        functools.partial(tail_kernel, HEAD ** (-0.5)),
        out_shape=(out, out),
        in_specs=[vmem] * 6,
        out_specs=(vmem, vmem),
        cost_estimate=pl.CostEstimate(
            flops=4 * HEADS * rows * HEAD * HEAD, transcendentals=0, bytes_accessed=12 * rows * 1024 * 4
        ),
    )(lower_later, upper_later, local_k, local_v, value, key)


def per_device(query, key, value, grad_out):
    rows_dev = query.shape[0]
    scaling = HEAD ** (-0.5)
    queries = query.reshape(rows_dev, HEADS, HEAD)
    key_rows = key.reshape(rows_dev, HEADS, HEAD)
    value_rows = value.reshape(rows_dev, HEADS, HEAD)
    line = lax.broadcasted_iota(jnp.int32, (rows_dev, rows_dev), 0)
    column = lax.broadcasted_iota(jnp.int32, (rows_dev, rows_dev), 1)
    causal = (line >= column)[None]
    state = jnp.einsum("thi,thj->hij", key_rows, value_rows, preferred_element_type=jnp.float32)
    prior = chunked_scan(state, False)
    prior_half = prior.astype(jnp.bfloat16)
    scores = (
        jnp.einsum("thi,shi->hts", queries, key_rows, preferred_element_type=jnp.float32) * scaling
    )
    score_half = jnp.where(causal, scores, 0.0).astype(jnp.bfloat16)
    attended = jnp.einsum(
        "hts,shj->thj", score_half, value_rows, preferred_element_type=jnp.float32
    )
    attended = attended + scaling * jnp.einsum(
        "thi,hij->thj", queries, prior_half, preferred_element_type=jnp.float32
    )
    flat = attended.reshape(rows_dev, HEADS * HEAD)
    inverse = lax.rsqrt(jnp.mean(flat * flat, axis=-1, keepdims=True) + 1e-05)
    normed = flat * inverse
    grads_flat = grad_out.astype(jnp.float32)
    grad_pre = inverse * (
        grads_flat - normed * jnp.mean(grads_flat * normed, axis=-1, keepdims=True)
    )
    grad_half = grad_pre.astype(jnp.bfloat16).reshape(rows_dev, HEADS, HEAD)
    dscores = jnp.einsum("thj,shj->hts", grad_half, value_rows, preferred_element_type=jnp.float32)
    dscore_half = jnp.where(causal, dscores, 0.0).astype(jnp.bfloat16)
    grad_q = jnp.einsum("hts,shi->thi", dscore_half, key_rows, preferred_element_type=jnp.float32)
    grad_q = scaling * (
        grad_q
        + jnp.einsum("thj,hij->thi", grad_half, prior_half, preferred_element_type=jnp.float32)
    )
    grad_state = jnp.einsum("thi,thj->hij", queries, grad_half, preferred_element_type=jnp.float32)
    lower_known, lower_got, upper_later = chunked_scan(grad_state, True)
    local_k = jnp.einsum("hts,thi->hsi", dscore_half, queries, preferred_element_type=jnp.float32)
    local_v = jnp.einsum("hts,thj->hsj", score_half, grad_half, preferred_element_type=jnp.float32)
    grad_k, grad_v = tail(lower_known + lower_got, upper_later, local_k, local_v, value, key)
    width = HEADS * HEAD
    return (
        normed.astype(jnp.bfloat16),
        grad_q.reshape(rows_dev, width).astype(jnp.bfloat16),
        grad_k,
        grad_v,
    )


def solution(mesh):
    placed = P(("grp", "outer", "inner"), None)
    return jax.shard_map(
        per_device,
        mesh=mesh,
        in_specs=(placed, placed, placed, placed),
        out_specs=(placed, placed, placed, placed),
        check_vma=False,
    )
```

```python
import functools

import jax
import jax.numpy as jnp
from jax import lax
from jax.experimental import pallas as pl
from jax.experimental.pallas import tpu as pltpu
from jax.sharding import PartitionSpec as P

HEADS = 8
HEAD = 128


def axis_bits(axis):
    count = lax.axis_size(axis)
    return [1 << k for k in range(count.bit_length() - 1)]


def swap(value, axis, bit):
    count = lax.axis_size(axis)
    return lax.ppermute(value, axis, [(i, i ^ bit) for i in range(count)])


def partner_counts(axis, bit, backward):
    partner_lower = (lax.axis_index(axis) & bit) != 0
    return jnp.logical_not(partner_lower) if backward else partner_lower


def subcube_step(earlier, total, axis, bit, backward):
    got = swap(total, axis, bit)
    counted = partner_counts(axis, bit, backward)
    return earlier + [jnp.where(counted, got, 0.0)], total + got


def added(pieces, like):
    total = jnp.zeros_like(like)
    for piece in pieces:
        total = total + piece
    return total


def scan_inner_first(value, backward):
    earlier, total = [], value
    for axis in ("inner", "outer"):
        for bit in axis_bits(axis):
            earlier, total = subcube_step(earlier, total, axis, bit, backward)
    return added(earlier, value)


def chunked_scan(value, backward):
    half = value.shape[0] // 2
    group_a, group_b = value[:half], value[half:]
    if backward:
        group_a, group_b = group_b, group_a
    inner_bits, outer_bits = axis_bits("inner"), axis_bits("outer")
    if not inner_bits:
        result = scan_inner_first(value, backward)
        if backward:
            return result[:half], jnp.zeros_like(result[:half]), result[half:]
        return result
    earlier_a, total_a = subcube_step([], group_a, "inner", inner_bits[0], backward)
    earlier_b, total_b = [], group_b
    for bit in inner_bits[1:]:
        earlier_b, total_b = subcube_step(earlier_b, total_b, "inner", bit, backward)
    if backward:
        (earlier_b, total_b), _ = lax.optimization_barrier(((earlier_b, total_b), total_a))
    rows_before, rows_total = [], total_b
    if not backward:
        (earlier_a, total_a), _ = lax.optimization_barrier(((earlier_a, total_a), rows_total))
    for bit in outer_bits:
        rows_before, rows_total = subcube_step(rows_before, rows_total, "outer", bit, backward)
    for bit in inner_bits[1:]:
        earlier_a, total_a = subcube_step(earlier_a, total_a, "inner", bit, backward)
    for bit in outer_bits:
        earlier_a, total_a = subcube_step(earlier_a, total_a, "outer", bit, backward)
    low = inner_bits[0]
    counted = partner_counts("inner", low, backward)
    known = added(rows_before + earlier_b, group_b)
    sent = jnp.where(counted, known, known + group_b)
    earlier_a = added(earlier_a, group_a)
    got_b = swap(sent, "inner", low)
    if backward:
        return known, got_b, earlier_a
    return jnp.concatenate([earlier_a, known + got_b], axis=0)


def tail_kernel(scaling, lower_later, upper_later, local_k, local_v, value, key, out_k, out_v):
    half = HEADS // 2
    for h in range(HEADS):
        later = lower_later[h] if h < half else upper_later[h - half]
        later_half = later.astype(jnp.bfloat16)
        cols = slice(h * HEAD, (h + 1) * HEAD)
        from_later_k = lax.dot_general(
            value[:, cols], later_half, (((1,), (1,)), ((), ())), preferred_element_type=jnp.float32
        )
        out_k[:, cols] = (scaling * (local_k[h] + from_later_k)).astype(out_k.dtype)
        from_later_v = lax.dot_general(
            key[:, cols], later_half, (((1,), (0,)), ((), ())), preferred_element_type=jnp.float32
        )
        out_v[:, cols] = (local_v[h] + scaling * from_later_v).astype(out_v.dtype)


def tail(lower_later, upper_later, local_k, local_v, value, key):
    rows = value.shape[0]
    vmem = pl.BlockSpec(memory_space=pltpu.VMEM)
    out = jax.ShapeDtypeStruct((rows, HEADS * HEAD), jnp.bfloat16)
    return pl.pallas_call(
        functools.partial(tail_kernel, HEAD ** (-0.5)),
        out_shape=(out, out),
        in_specs=[vmem] * 6,
        out_specs=(vmem, vmem),
        cost_estimate=pl.CostEstimate(
            flops=4 * HEADS * rows * HEAD * HEAD, transcendentals=0, bytes_accessed=12 * rows * 1024 * 4
        ),
    )(lower_later, upper_later, local_k, local_v, value, key)


def per_device(query, key, value, grad_out):
    rows_dev = query.shape[0]
    scaling = HEAD ** (-0.5)
    queries = query.reshape(rows_dev, HEADS, HEAD)
    key_rows = key.reshape(rows_dev, HEADS, HEAD)
    value_rows = value.reshape(rows_dev, HEADS, HEAD)
    line = lax.broadcasted_iota(jnp.int32, (rows_dev, rows_dev), 0)
    column = lax.broadcasted_iota(jnp.int32, (rows_dev, rows_dev), 1)
    causal = (line >= column)[None]
    state = jnp.einsum("thi,thj->hij", key_rows, value_rows, preferred_element_type=jnp.float32)
    prior = chunked_scan(state, False)
    prior_half = prior.astype(jnp.bfloat16)
    scores = (
        jnp.einsum("thi,shi->hts", queries, key_rows, preferred_element_type=jnp.float32) * scaling
    )
    score_half = jnp.where(causal, scores, 0.0).astype(jnp.bfloat16)
    attended = jnp.einsum(
        "hts,shj->thj", score_half, value_rows, preferred_element_type=jnp.float32
    )
    attended = attended + scaling * jnp.einsum(
        "thi,hij->thj", queries, prior_half, preferred_element_type=jnp.float32
    )
    flat = attended.reshape(rows_dev, HEADS * HEAD)
    inverse = lax.rsqrt(jnp.mean(flat * flat, axis=-1, keepdims=True) + 1e-05)
    normed = flat * inverse
    grads_flat = grad_out.astype(jnp.float32)
    grad_pre = inverse * (
        grads_flat - normed * jnp.mean(grads_flat * normed, axis=-1, keepdims=True)
    )
    grad_half = grad_pre.astype(jnp.bfloat16).reshape(rows_dev, HEADS, HEAD)
    dscores = jnp.einsum("thj,shj->hts", grad_half, value_rows, preferred_element_type=jnp.float32)
    dscore_half = jnp.where(causal, dscores, 0.0).astype(jnp.bfloat16)
    grad_q = jnp.einsum("hts,shi->thi", dscore_half, key_rows, preferred_element_type=jnp.float32)
    grad_q = scaling * (
        grad_q
        + jnp.einsum("thj,hij->thi", grad_half, prior_half, preferred_element_type=jnp.float32)
    )
    grad_state = jnp.einsum("thi,thj->hij", queries, grad_half, preferred_element_type=jnp.float32)
    lower_known, lower_got, upper_later = chunked_scan(grad_state, True)
    local_k = jnp.einsum("hts,thi->hsi", dscore_half, queries, preferred_element_type=jnp.float32)
    local_v = jnp.einsum("hts,thj->hsj", score_half, grad_half, preferred_element_type=jnp.float32)
    grad_k, grad_v = tail(lower_known + lower_got, upper_later, local_k, local_v, value, key)
    width = HEADS * HEAD
    return (
        normed.astype(jnp.bfloat16),
        grad_q.reshape(rows_dev, width).astype(jnp.bfloat16),
        grad_k,
        grad_v,
    )


def solution(mesh):
    placed = P(("grp", "outer", "inner"), None)
    return jax.shard_map(
        per_device,
        mesh=mesh,
        in_specs=(placed, placed, placed, placed),
        out_specs=(placed, placed, placed, placed),
        check_vma=False,
    )
```

```python
import functools

import jax
import jax.numpy as jnp
from jax import lax
from jax.experimental import pallas as pl
from jax.experimental.pallas import tpu as pltpu
from jax.sharding import PartitionSpec as P

HEADS = 8
HEAD = 128


def axis_bits(axis):
    count = lax.axis_size(axis)
    return [1 << k for k in range(count.bit_length() - 1)]


def swap(value, axis, bit):
    count = lax.axis_size(axis)
    return lax.ppermute(value, axis, [(i, i ^ bit) for i in range(count)])


def partner_counts(axis, bit, backward):
    partner_lower = (lax.axis_index(axis) & bit) != 0
    return jnp.logical_not(partner_lower) if backward else partner_lower


def subcube_step(earlier, total, axis, bit, backward):
    got = swap(total, axis, bit)
    counted = partner_counts(axis, bit, backward)
    return earlier + [jnp.where(counted, got, 0.0)], total + got


def added(pieces, like):
    total = jnp.zeros_like(like)
    for piece in pieces:
        total = total + piece
    return total


def scan_inner_first(value, backward):
    earlier, total = [], value
    for axis in ("inner", "outer"):
        for bit in axis_bits(axis):
            earlier, total = subcube_step(earlier, total, axis, bit, backward)
    return added(earlier, value)


def chunked_scan(value, backward):
    half = value.shape[0] // 2
    group_a, group_b = value[:half], value[half:]
    if backward:
        group_a, group_b = group_b, group_a
    inner_bits, outer_bits = axis_bits("inner"), axis_bits("outer")
    if not inner_bits:
        result = scan_inner_first(value, backward)
        if backward:
            return result[:half], jnp.zeros_like(result[:half]), result[half:]
        return result
    earlier_a, total_a = subcube_step([], group_a, "inner", inner_bits[0], backward)
    earlier_b, total_b = [], group_b
    for bit in inner_bits[1:]:
        earlier_b, total_b = subcube_step(earlier_b, total_b, "inner", bit, backward)
    if backward:
        (earlier_b, total_b), _ = lax.optimization_barrier(((earlier_b, total_b), total_a))
    rows_before, rows_total = [], total_b
    if not backward:
        (earlier_a, total_a), _ = lax.optimization_barrier(((earlier_a, total_a), rows_total))
    for bit in outer_bits:
        rows_before, rows_total = subcube_step(rows_before, rows_total, "outer", bit, backward)
    for bit in inner_bits[1:]:
        earlier_a, total_a = subcube_step(earlier_a, total_a, "inner", bit, backward)
    for bit in outer_bits:
        earlier_a, total_a = subcube_step(earlier_a, total_a, "outer", bit, backward)
    low = inner_bits[0]
    counted = partner_counts("inner", low, backward)
    ready = lax.optimization_barrier(added(rows_before[:-1] + earlier_b, group_b))
    known = ready + rows_before[-1]
    sent = jnp.where(counted, ready, ready + group_b) + rows_before[-1]
    earlier_a = added(earlier_a, group_a)
    got_b = swap(sent, "inner", low)
    if backward:
        return known, got_b, earlier_a
    return jnp.concatenate([earlier_a, known + got_b], axis=0)


def tail_kernel(scaling, lower_later, upper_later, local_k, local_v, value, key, out_k, out_v):
    half = HEADS // 2
    for h in range(HEADS):
        later = lower_later[h] if h < half else upper_later[h - half]
        later_half = later.astype(jnp.bfloat16)
        cols = slice(h * HEAD, (h + 1) * HEAD)
        from_later_k = lax.dot_general(
            value[:, cols], later_half, (((1,), (1,)), ((), ())), preferred_element_type=jnp.float32
        )
        out_k[:, cols] = (scaling * (local_k[h] + from_later_k)).astype(out_k.dtype)
        from_later_v = lax.dot_general(
            key[:, cols], later_half, (((1,), (0,)), ((), ())), preferred_element_type=jnp.float32
        )
        out_v[:, cols] = (local_v[h] + scaling * from_later_v).astype(out_v.dtype)


def tail(lower_later, upper_later, local_k, local_v, value, key):
    rows = value.shape[0]
    vmem = pl.BlockSpec(memory_space=pltpu.VMEM)
    out = jax.ShapeDtypeStruct((rows, HEADS * HEAD), jnp.bfloat16)
    return pl.pallas_call(
        functools.partial(tail_kernel, HEAD ** (-0.5)),
        out_shape=(out, out),
        in_specs=[vmem] * 6,
        out_specs=(vmem, vmem),
        cost_estimate=pl.CostEstimate(
            flops=4 * HEADS * rows * HEAD * HEAD, transcendentals=0, bytes_accessed=12 * rows * 1024 * 4
        ),
    )(lower_later, upper_later, local_k, local_v, value, key)


def per_device(query, key, value, grad_out):
    rows_dev = query.shape[0]
    scaling = HEAD ** (-0.5)
    queries = query.reshape(rows_dev, HEADS, HEAD)
    key_rows = key.reshape(rows_dev, HEADS, HEAD)
    value_rows = value.reshape(rows_dev, HEADS, HEAD)
    line = lax.broadcasted_iota(jnp.int32, (rows_dev, rows_dev), 0)
    column = lax.broadcasted_iota(jnp.int32, (rows_dev, rows_dev), 1)
    causal = (line >= column)[None]
    state = jnp.einsum("thi,thj->hij", key_rows, value_rows, preferred_element_type=jnp.float32)
    prior = chunked_scan(state, False)
    prior_half = prior.astype(jnp.bfloat16)
    scores = (
        jnp.einsum("thi,shi->hts", queries, key_rows, preferred_element_type=jnp.float32) * scaling
    )
    score_half = jnp.where(causal, scores, 0.0).astype(jnp.bfloat16)
    attended = jnp.einsum(
        "hts,shj->thj", score_half, value_rows, preferred_element_type=jnp.float32
    )
    attended = attended + scaling * jnp.einsum(
        "thi,hij->thj", queries, prior_half, preferred_element_type=jnp.float32
    )
    flat = attended.reshape(rows_dev, HEADS * HEAD)
    inverse = lax.rsqrt(jnp.mean(flat * flat, axis=-1, keepdims=True) + 1e-05)
    normed = flat * inverse
    grads_flat = grad_out.astype(jnp.float32)
    grad_pre = inverse * (
        grads_flat - normed * jnp.mean(grads_flat * normed, axis=-1, keepdims=True)
    )
    grad_half = grad_pre.astype(jnp.bfloat16).reshape(rows_dev, HEADS, HEAD)
    dscores = jnp.einsum("thj,shj->hts", grad_half, value_rows, preferred_element_type=jnp.float32)
    dscore_half = jnp.where(causal, dscores, 0.0).astype(jnp.bfloat16)
    grad_q = jnp.einsum("hts,shi->thi", dscore_half, key_rows, preferred_element_type=jnp.float32)
    grad_q = scaling * (
        grad_q
        + jnp.einsum("thj,hij->thi", grad_half, prior_half, preferred_element_type=jnp.float32)
    )
    grad_state = jnp.einsum("thi,thj->hij", queries, grad_half, preferred_element_type=jnp.float32)
    lower_known, lower_got, upper_later = chunked_scan(grad_state, True)
    local_k = jnp.einsum("hts,thi->hsi", dscore_half, queries, preferred_element_type=jnp.float32)
    local_v = jnp.einsum("hts,thj->hsj", score_half, grad_half, preferred_element_type=jnp.float32)
    grad_k, grad_v = tail(lower_known + lower_got, upper_later, local_k, local_v, value, key)
    width = HEADS * HEAD
    return (
        normed.astype(jnp.bfloat16),
        grad_q.reshape(rows_dev, width).astype(jnp.bfloat16),
        grad_k,
        grad_v,
    )


def solution(mesh):
    placed = P(("grp", "outer", "inner"), None)
    return jax.shard_map(
        per_device,
        mesh=mesh,
        in_specs=(placed, placed, placed, placed),
        out_specs=(placed, placed, placed, placed),
        check_vma=False,
    )
```
